128 devices in a mesh: dp: 4 (over z), outer: 16 (over x, y), inner: 2 (over core).
Axes of the slice: x: 4, y: 4, z: 4, core: 2. Of those that a mesh axis runs over, the one named last changes fastest.
Arguments:
- tokens: bfloat16 [4096, 4096], P(('dp', 'outer', 'inner')), may hold values from -6 to 6
- expert_ids: int32 [4096, 8], P(('dp', 'outer', 'inner')), may hold values from 0 to 31, all different within a row; in each aligned block of 32 rows (0 to 31, 32 to 63, ...) at most 12 rows name the same one
- gate_values: float32 [4096, 8], P(('dp', 'outer', 'inner')), may hold values from 0.02 to 0.5
- upstream: bfloat16 [4096, 4096], P(('dp', 'outer', 'inner')), may hold values from -1.5 to 1.5
- w_gate: bfloat16 [32, 4096, 768], P(('outer', 'inner')), may hold values from -0.09375 to 0.09375
- w_up: bfloat16 [32, 4096, 768], P(('outer', 'inner')), may hold values from -0.09375 to 0.09375
- w_down: bfloat16 [32, 768, 4096], P(('outer', 'inner')), may hold values from -0.21875 to 0.21875
Outputs:
- output: bfloat16 [4096, 4096], P(('dp', 'outer', 'inner'))
- grad_tokens: bfloat16 [4096, 4096], P(('dp', 'outer', 'inner'))
- grad_gates: float32 [4096, 8], P(('dp', 'outer', 'inner'))
- grad_w_gate: bfloat16 [32, 4096, 768], P(('outer', 'inner'), 'dp')
- grad_w_up: bfloat16 [32, 4096, 768], P(('outer', 'inner'), 'dp')
- grad_w_down: bfloat16 [32, 768, 4096], P(('outer', 'inner'), None, 'dp')
The draws below stay inside these ranges and needn't reach their ends.
Inputs may be any that keep to these rules, and one draw needn't show every extreme that they name: `expert_ids`: each token names 8 different experts. Among the 32 tokens of one device (aligned blocks of rows), no expert is named more than 12 times, a bound that some block reaches.
All inputs are finite; a program needn't handle non-finite values.
Results may differ from the reference program's by a relative error of at most 0.013.
Values may be sent and summed in bfloat16 or wider, within the bound.
No kernel may reach another device: no remote copies, remote signals or barrier semaphores. Data moves between devices by JAX's collectives and lax.ppermute only.
A program may use at most 192 MiB of HBM per device.

```python
import math
import jax
import jax.numpy as jnp
import numpy as np
from jax import lax

D = 4096
TOP = 8
FF = 768
TOK_DEV = 32
EXPERTS = 32
TOKENS = 4096
CAP = 12
N_DP = 4


def shard_levels(stream_key, dims, cuts, smallest, high):
    gain = 1.0
    for axis_at, blocks in cuts:
        draws = jax.random.uniform(jax.random.fold_in(jax.random.fold_in(stream_key, 6), axis_at), (blocks,), jnp.float32, smallest / len(cuts), high / len(cuts))
        gain = gain * jnp.repeat(jnp.exp(draws), dims[axis_at] // blocks).reshape((-1,) + (1,) * (len(dims) - 1 - axis_at))
    return gain


def deal_out(key, own, number, rows, number_of, top, reach, skew):
    order = jax.random.permutation(key, number_of)
    packed, usual = portions_of(number_of, rows * top, reach, skew, True), portions_of(number_of, rows * top, reach, skew, False)
    places = jnp.arange(number_of)

    def named(sizes, turn):
        used = int((sizes > 0).sum())
        fixed = max(1, used // 4)
        moved = fixed + (places - fixed + turn * (used - fixed)) % max(1, number_of - fixed)
        return jnp.zeros((number_of,), jnp.int32).at[order[jnp.where(places < fixed, places, moved)]].set(jnp.asarray(sizes, jnp.int32))

    sizes = jnp.where(number % 4 == 0, named(packed, number // 4), named(usual, number - number // 4 - 1))
    mixed = jax.random.permutation(jax.random.fold_in(own, 3), number_of)
    source_of, receiver = mixed[0:number_of // 2 * 2:2], mixed[1:number_of // 2 * 2:2]
    room = jnp.minimum(sizes[source_of] - 1, reach - sizes[receiver]) // 2
    room = jnp.where((source_of == order[0]) | (receiver == order[0]) | (sizes[receiver] == 0), 0, jnp.maximum(room, 0))
    moved = jax.random.randint(jax.random.fold_in(own, 4), (number_of // 2,), 0, 1 << 20) % (room + 1)
    sizes = sizes.at[source_of].add(-moved).at[receiver].add(moved)
    items = jnp.searchsorted(jnp.cumsum(sizes), jnp.arange(rows * top), side="right").astype(jnp.int32)
    listing = items.reshape(top, rows).T
    listing = listing[jax.random.permutation(jax.random.fold_in(own, 1), rows)]
    turn = jax.random.randint(jax.random.fold_in(own, 2), (rows, 1), 0, top)
    return jnp.take_along_axis(listing, (jnp.arange(top)[None, :] + turn) % top, axis=1)


def portions_of(count, total, bound, skew, full):
    portions = [(1 << 20) // math.isqrt(grade ** skew) + 1 for grade in range(1, count + 1)]
    largest = bound if full else min(bound, max(-(-total // count), total * portions[0] // sum(portions)))
    least = 1 if total - largest >= count - 1 else 0
    given, surplus = [largest] + [least] * (count - 1), total - largest - least * (count - 1)
    while surplus > 0:
        candidates = [i for i in range(1, count) if given[i] < largest] or [i for i in range(1, count) if given[i] < bound]
        pool, budget = sum([portions[i] for i in candidates]), surplus
        for i in candidates:
            more = min(bound - given[i], max(1, budget * portions[i] // pool), surplus)
            given[i] = given[i] + more
            surplus = surplus - more
    return np.array(given)


def gaussian(own_key, dims, spread, most, pieces=(), held_as=jnp.bfloat16):
    values = jax.random.normal(own_key, dims, jnp.float32) * spread
    if len(pieces) > 0:
        values = shard_levels(own_key, dims, pieces, -0.22, 0.18) * values
    return jnp.clip(values, min=-most, max=most).astype(held_as)


def setup_inputs(seed: int = 0) -> dict:
    streams_of = jax.random.split(jax.random.key(seed), 8)
    tokens = gaussian(streams_of[0], (TOKENS, D), 1.0, 6.0, ((0, 128),))
    expert_ids_keys = jax.random.split(jax.random.fold_in(streams_of[1], 1), TOKENS // TOK_DEV)
    expert_ids_turns = jax.random.permutation(jax.random.fold_in(streams_of[1], 3), TOKENS // TOK_DEV)
    expert_ids = jax.vmap(lambda own, number: deal_out(jax.random.fold_in(streams_of[1], 2), own, number, TOK_DEV, EXPERTS, TOP, CAP, 1))(expert_ids_keys, expert_ids_turns).reshape((TOKENS, TOP))
    gate_values = jnp.clip(jnp.exp(math.log(0.5) - 3.218876 * jax.random.uniform(streams_of[2], (TOKENS, TOP), jnp.float32) ** shard_levels(streams_of[2], (TOKENS, TOP), ((0, 128),), -0.2, 0.2)), 0.02, 0.5)
    upstream = gaussian(streams_of[3], (TOKENS, D), 0.25, 1.5, ((0, 128),))
    w_gate = gaussian(streams_of[4], (EXPERTS, D, FF), D ** -0.5, 0.09375, ((0, 32),))
    w_up = gaussian(streams_of[5], (EXPERTS, D, FF), D ** -0.5, 0.09375, ((0, 32),))
    w_down = gaussian(streams_of[6], (EXPERTS, FF, D), FF ** -0.5, 0.21875, ((0, 32),))
    return dict(tokens=tokens, expert_ids=expert_ids, gate_values=gate_values, upstream=upstream, w_gate=w_gate, w_up=w_up, w_down=w_down)


block_rows = 64


def contract_last(left, right):
    return lax.dot_general(left, right, (((1,), (1,)), ((), ())), preferred_element_type=jnp.float32)


def contract_first(left, right):
    return lax.dot_general(left, right, (((0,), (0,)), ((), ())), preferred_element_type=jnp.float32)


def expert_rows(rows_in, grads_in, gate_mat, up_mat, down_mat):
    gate_pre = jnp.dot(rows_in, gate_mat, preferred_element_type=jnp.float32)
    up_pre = jnp.dot(rows_in, up_mat, preferred_element_type=jnp.float32)
    sigma = jax.nn.sigmoid(gate_pre)
    silu_value = gate_pre * sigma
    hidden = (silu_value * up_pre).astype(jnp.bfloat16)
    expert_out = jnp.dot(hidden, down_mat, preferred_element_type=jnp.float32).astype(jnp.bfloat16)
    grad_hidden = contract_last(grads_in, down_mat)
    slope = sigma * (1.0 + gate_pre * (1.0 - sigma))
    grad_gate_pre = (grad_hidden * up_pre * slope).astype(jnp.bfloat16)
    grad_up_pre = (grad_hidden * silu_value).astype(jnp.bfloat16)
    pair_grad = (contract_last(grad_gate_pre, gate_mat) + contract_last(grad_up_pre, up_mat)).astype(jnp.bfloat16)
    return hidden, expert_out, grad_gate_pre, grad_up_pre, pair_grad


def reference(tokens, expert_ids, gate_values, upstream, w_gate, w_up, w_down):
    group_tokens = TOKENS // N_DP
    group_pairs = group_tokens * TOP
    padded_rows = group_pairs + EXPERTS * block_rows
    block_count = padded_rows // block_rows
    total_gate = jnp.zeros((EXPERTS, D, FF), jnp.float32)
    total_up = jnp.zeros((EXPERTS, D, FF), jnp.float32)
    total_down = jnp.zeros((EXPERTS, FF, D), jnp.float32)
    out_list = []
    grad_list = []
    gate_grad_list = []
    for group in range(N_DP):
        first = group * group_tokens
        group_tok = tokens[first:first + group_tokens]
        group_up = upstream[first:first + group_tokens]
        flat_ids = expert_ids[first:first + group_tokens].reshape(-1)
        flat_gates = gate_values[first:first + group_tokens].reshape(-1)
        expert_iota = jnp.arange(EXPERTS, dtype=jnp.int32)
        counts = jnp.sum((flat_ids[:, None] == expert_iota[None, :]).astype(jnp.int32), axis=0)
        padded = (counts + block_rows - 1) // block_rows * block_rows
        pad_start = (jnp.cumsum(padded) - padded).astype(jnp.int32)
        plain_start = (jnp.cumsum(counts) - counts).astype(jnp.int32)
        order = jnp.argsort(flat_ids, stable=True).astype(jnp.int32)
        sorted_ids = flat_ids[order]
        position = (pad_start[sorted_ids] + jnp.arange(group_pairs, dtype=jnp.int32) - plain_start[sorted_ids]).astype(jnp.int32)
        slot_pair = jnp.full((padded_rows,), group_pairs, jnp.int32).at[position].set(order)
        pair_slot = jnp.zeros((group_pairs,), jnp.int32).at[order].set(position)
        block_first = jnp.arange(block_count, dtype=jnp.int32) * block_rows
        block_expert = jnp.clip(jnp.sum((pad_start[None, :] <= block_first[:, None]).astype(jnp.int32), axis=1) - 1, 0, EXPERTS - 1).astype(jnp.int32)
        pair_token = jnp.arange(group_pairs, dtype=jnp.int32) // TOP
        scaled = (flat_gates[:, None] * group_up[pair_token].astype(jnp.float32)).astype(jnp.bfloat16)
        token_pad = jnp.concatenate([group_tok, jnp.zeros((1, D), jnp.bfloat16)], axis=0)
        scaled_pad = jnp.concatenate([scaled, jnp.zeros((1, D), jnp.bfloat16)], axis=0)
        slot_token = jnp.where(slot_pair < group_pairs, slot_pair // TOP, group_tokens).astype(jnp.int32)

        def visit(carry, block_index):
            start = block_index * block_rows
            expert = block_expert[block_index]
            rows_in = token_pad[lax.dynamic_slice_in_dim(slot_token, start, block_rows)]
            grads_in = scaled_pad[lax.dynamic_slice_in_dim(slot_pair, start, block_rows)]
            hidden, expert_out, grad_gate_pre, grad_up_pre, pair_grad = expert_rows(
                rows_in, grads_in, w_gate[expert], w_up[expert], w_down[expert])
            part_gate, part_up, part_down = carry
            part_gate = part_gate.at[expert].add(contract_first(rows_in, grad_gate_pre))
            part_up = part_up.at[expert].add(contract_first(rows_in, grad_up_pre))
            part_down = part_down.at[expert].add(contract_first(hidden, grads_in))
            return (part_gate, part_up, part_down), (expert_out, pair_grad)

        start_parts = (jnp.zeros((EXPERTS, D, FF), jnp.float32), jnp.zeros((EXPERTS, D, FF), jnp.float32),
                       jnp.zeros((EXPERTS, FF, D), jnp.float32))
        parts, (block_out, block_grad) = lax.scan(visit, start_parts, jnp.arange(block_count, dtype=jnp.int32))
        total_gate = total_gate + lax.optimization_barrier(parts[0].astype(jnp.bfloat16)).astype(jnp.float32)
        total_up = total_up + lax.optimization_barrier(parts[1].astype(jnp.bfloat16)).astype(jnp.float32)
        total_down = total_down + lax.optimization_barrier(parts[2].astype(jnp.bfloat16)).astype(jnp.float32)
        pair_out = block_out.reshape(padded_rows, D)[pair_slot].reshape(group_tokens, TOP, D).astype(jnp.float32)
        pair_back = block_grad.reshape(padded_rows, D)[pair_slot].reshape(group_tokens, TOP, D).astype(jnp.float32)
        gates_grid = flat_gates.reshape(group_tokens, TOP)
        out_list.append(jnp.sum(gates_grid[:, :, None] * pair_out, axis=1).astype(jnp.bfloat16))
        grad_list.append(jnp.sum(pair_back, axis=1).astype(jnp.bfloat16))
        gate_grad_list.append(jnp.einsum("tkd,td->tk", pair_out, group_up.astype(jnp.float32)))
    output = jnp.concatenate(out_list, axis=0)
    grad_tokens = jnp.concatenate(grad_list, axis=0)
    grad_gates = jnp.concatenate(gate_grad_list, axis=0)
    return (output, grad_tokens, grad_gates, total_gate.astype(jnp.bfloat16),
            total_up.astype(jnp.bfloat16), total_down.astype(jnp.bfloat16))
```

```python
import jax
import jax.numpy as jnp
from jax import lax
from jax.sharding import PartitionSpec as P


def contract_last(left, right):
    return lax.dot_general(
        left, right, (((1,), (1,)), ((), ())), preferred_element_type=jnp.float32
    )


def contract_first(left, right):
    return lax.dot_general(
        left, right, (((0,), (0,)), ((), ())), preferred_element_type=jnp.float32
    )


def expert_rows(rows_in, grads_in, gate_mat, up_mat, down_mat):
    gate_pre = jnp.dot(rows_in, gate_mat, preferred_element_type=jnp.float32)
    up_pre = jnp.dot(rows_in, up_mat, preferred_element_type=jnp.float32)
    sigma = jax.nn.sigmoid(gate_pre)
    silu_value = gate_pre * sigma
    hidden = (silu_value * up_pre).astype(jnp.bfloat16)
    expert_out = jnp.dot(hidden, down_mat, preferred_element_type=jnp.float32).astype(jnp.bfloat16)
    grad_hidden = contract_last(grads_in, down_mat)
    slope = sigma * (1.0 + gate_pre * (1.0 - sigma))
    grad_gate_pre = (grad_hidden * up_pre * slope).astype(jnp.bfloat16)
    grad_up_pre = (grad_hidden * silu_value).astype(jnp.bfloat16)
    pair_grad = (
        contract_last(grad_gate_pre, gate_mat) + contract_last(grad_up_pre, up_mat)
    ).astype(jnp.bfloat16)
    return (hidden, expert_out, grad_gate_pre, grad_up_pre, pair_grad)


def local(tokens, expert_ids, gate_values, upstream, w_gate, w_up, w_down):
    local_tokens = tokens.shape[0]
    width = tokens.shape[1]
    top_count = expert_ids.shape[1]
    ff_width = w_gate.shape[2]
    outer_count = lax.axis_size("outer")
    inner_count = lax.axis_size("inner")
    expert_count = outer_count * inner_count
    capacity = min(local_tokens, 3 * local_tokens * top_count // (2 * expert_count))
    pair_count = local_tokens * top_count
    flat_ids = expert_ids.reshape(-1)
    flat_gates = gate_values.reshape(-1)
    onehot = (flat_ids[:, None] == jnp.arange(expert_count, dtype=jnp.int32)[None, :]).astype(
        jnp.int32
    )
    slot_rank = jnp.sum((jnp.cumsum(onehot, axis=0) - onehot) * onehot, axis=1)
    pair_slot = flat_ids * capacity + slot_rank
    slot_pair = (
        jnp.full((expert_count * capacity,), pair_count, jnp.int32)
        .at[pair_slot]
        .set(jnp.arange(pair_count, dtype=jnp.int32))
    )
    slot_token = jnp.where(slot_pair < pair_count, slot_pair // top_count, local_tokens)
    token_pad = jnp.concatenate([tokens, jnp.zeros((1, width), jnp.bfloat16)], axis=0)
    upstream_pad = jnp.concatenate([upstream, jnp.zeros((1, width), jnp.bfloat16)], axis=0)
    gate_pad = jnp.concatenate([flat_gates, jnp.zeros((1,), jnp.float32)], axis=0)
    send_rows = token_pad[slot_token]
    send_grads = (
        gate_pad[slot_pair][:, None] * upstream_pad[slot_token].astype(jnp.float32)
    ).astype(jnp.bfloat16)
    flat_shape = (expert_count, capacity, width)
    got_rows, got_grads = (
        lax.all_to_all(
            send_rows.reshape(flat_shape),
            ("outer", "inner"),
            split_axis=0,
            concat_axis=0,
            tiled=True,
        ),
        lax.all_to_all(
            send_grads.reshape(flat_shape),
            ("outer", "inner"),
            split_axis=0,
            concat_axis=0,
            tiled=True,
        ),
    )
    rows_in = got_rows.reshape(-1, width)
    grads_in = got_grads.reshape(-1, width)
    hidden, expert_out, grad_gate_pre, grad_up_pre, pair_grad = expert_rows(
        rows_in, grads_in, w_gate[0], w_up[0], w_down[0]
    )
    back_out, back_grad = (
        lax.all_to_all(
            expert_out.reshape(flat_shape),
            ("outer", "inner"),
            split_axis=0,
            concat_axis=0,
            tiled=True,
        ),
        lax.all_to_all(
            pair_grad.reshape(flat_shape),
            ("outer", "inner"),
            split_axis=0,
            concat_axis=0,
            tiled=True,
        ),
    )
    dp_count = lax.axis_size("dp")
    slot_total = rows_in.shape[0]
    piece = width // dp_count

    def spread_columns(block):
        return lax.all_to_all(
            block.reshape(slot_total, dp_count, piece), "dp", split_axis=1, concat_axis=0, tiled=True
        ).reshape(dp_count * slot_total, piece)

    joined_grads = jnp.concatenate([grad_gate_pre, grad_up_pre], axis=1)
    rows_all = spread_columns(rows_in)
    grads_all = spread_columns(grads_in)
    joined_all = lax.all_gather(joined_grads, "dp", axis=0, tiled=True)
    hidden_all = lax.all_gather(hidden, "dp", axis=0, tiled=True)
    grad_joined = contract_first(rows_all, joined_all)
    grad_down = contract_first(hidden_all, grads_all)
    pair_out = back_out.reshape(-1, width)[pair_slot].reshape(local_tokens, top_count, width)
    pair_back = back_grad.reshape(-1, width)[pair_slot].reshape(local_tokens, top_count, width)
    output = jnp.sum(gate_values[:, :, None] * pair_out.astype(jnp.float32), axis=1).astype(
        jnp.bfloat16
    )
    grad_tokens = jnp.sum(pair_back.astype(jnp.float32), axis=1).astype(jnp.bfloat16)
    grad_gates = jnp.einsum("tkd,td->tk", pair_out, upstream, preferred_element_type=jnp.float32)
    grad_w_gate = grad_joined[:, :ff_width].astype(jnp.bfloat16)[None]
    grad_w_up = grad_joined[:, ff_width:].astype(jnp.bfloat16)[None]
    grad_w_down = grad_down.astype(jnp.bfloat16)[None]
    return (output, grad_tokens, grad_gates, grad_w_gate, grad_w_up, grad_w_down)


def solution(mesh):
    placed = (
        P(("dp", "outer", "inner"), None),
        P(("dp", "outer", "inner"), None),
        P(("dp", "outer", "inner"), None),
        P(("dp", "outer", "inner"), None),
        P(("outer", "inner"), None, None),
        P(("outer", "inner"), None, None),
        P(("outer", "inner"), None, None),
    )
    return jax.shard_map(
        local,
        mesh=mesh,
        in_specs=placed,
        out_specs=(
            P(("dp", "outer", "inner"), None),
            P(("dp", "outer", "inner"), None),
            P(("dp", "outer", "inner"), None),
            P(("outer", "inner"), "dp", None),
            P(("outer", "inner"), "dp", None),
            P(("outer", "inner"), None, "dp"),
        ),
        check_vma=False,
    )
```

```python
import jax
import jax.numpy as jnp
from jax import lax
from jax.sharding import PartitionSpec as P


def contract_last(left, right):
    return lax.dot_general(
        left, right, (((1,), (1,)), ((), ())), preferred_element_type=jnp.float32
    )


def contract_first(left, right):
    return lax.dot_general(
        left, right, (((0,), (0,)), ((), ())), preferred_element_type=jnp.float32
    )


def expert_rows(rows_in, grads_in, gate_mat, up_mat, down_mat):
    gate_pre = jnp.dot(rows_in, gate_mat, preferred_element_type=jnp.float32)
    up_pre = jnp.dot(rows_in, up_mat, preferred_element_type=jnp.float32)
    sigma = jax.nn.sigmoid(gate_pre)
    silu_value = gate_pre * sigma
    hidden = (silu_value * up_pre).astype(jnp.bfloat16)
    expert_out = jnp.dot(hidden, down_mat, preferred_element_type=jnp.float32).astype(jnp.bfloat16)
    grad_hidden = contract_last(grads_in, down_mat)
    slope = sigma * (1.0 + gate_pre * (1.0 - sigma))
    grad_gate_pre = (grad_hidden * up_pre * slope).astype(jnp.bfloat16)
    grad_up_pre = (grad_hidden * silu_value).astype(jnp.bfloat16)
    pair_grad = (
        contract_last(grad_gate_pre, gate_mat) + contract_last(grad_up_pre, up_mat)
    ).astype(jnp.bfloat16)
    return (hidden, expert_out, grad_gate_pre, grad_up_pre, pair_grad)


def local(tokens, expert_ids, gate_values, upstream, w_gate, w_up, w_down):
    local_tokens = tokens.shape[0]
    width = tokens.shape[1]
    top_count = expert_ids.shape[1]
    ff_width = w_gate.shape[2]
    outer_count = lax.axis_size("outer")
    inner_count = lax.axis_size("inner")
    dp_count = lax.axis_size("dp")
    expert_count = outer_count * inner_count
    group = ("outer", "inner")
    me = lax.axis_index("outer") * inner_count + lax.axis_index("inner")
    group_tokens = expert_count * local_tokens
    capacity = min(local_tokens, 3 * local_tokens * top_count // (2 * expert_count))
    slot_total = expert_count * capacity

    ids_all = lax.all_gather(expert_ids, group, axis=0, tiled=True)
    gates_all = lax.all_gather(gate_values, group, axis=0, tiled=True)
    tokens_all = lax.all_gather(tokens, group, axis=0, tiled=True)
    upstream_all = lax.all_gather(upstream, group, axis=0, tiled=True)

    chosen = ids_all == me
    picked = jnp.any(chosen, axis=1)
    token_gate = jnp.sum(jnp.where(chosen, gates_all, 0.0), axis=1)
    position = jnp.cumsum(picked.astype(jnp.int32)) - 1
    token_slot = jnp.where(picked, position, slot_total)
    slot_token = (
        jnp.full((slot_total + 1,), group_tokens, jnp.int32)
        .at[token_slot]
        .set(jnp.arange(group_tokens, dtype=jnp.int32))[:slot_total]
    )
    token_pad = jnp.concatenate([tokens_all, jnp.zeros((1, width), jnp.bfloat16)], axis=0)
    upstream_pad = jnp.concatenate([upstream_all, jnp.zeros((1, width), jnp.bfloat16)], axis=0)
    gate_pad = jnp.concatenate([token_gate, jnp.zeros((1,), jnp.float32)], axis=0)
    rows_in = token_pad[slot_token]
    up_rows = upstream_pad[slot_token]
    grads_in = (gate_pad[slot_token][:, None] * up_rows.astype(jnp.float32)).astype(jnp.bfloat16)

    hidden, expert_out, grad_gate_pre, grad_up_pre, pair_grad = expert_rows(
        rows_in, grads_in, w_gate[0], w_up[0], w_down[0]
    )

    slot_gates_grad = jnp.sum(
        up_rows.astype(jnp.float32) * expert_out.astype(jnp.float32), axis=1
    )
    out_pad = jnp.concatenate([expert_out, jnp.zeros((1, width), jnp.bfloat16)], axis=0)
    back_pad = jnp.concatenate([pair_grad, jnp.zeros((1, width), jnp.bfloat16)], axis=0)
    gg_pad = jnp.concatenate([slot_gates_grad, jnp.zeros((1,), jnp.float32)], axis=0)
    out_share = (token_gate[:, None] * out_pad[token_slot].astype(jnp.float32)).astype(jnp.bfloat16)
    back_share = back_pad[token_slot]
    gg_share = jnp.where(chosen, gg_pad[token_slot][:, None], 0.0)
    output = lax.psum_scatter(out_share, group, scatter_dimension=0, tiled=True)
    grad_tokens = lax.psum_scatter(back_share, group, scatter_dimension=0, tiled=True)
    grad_gates = lax.psum_scatter(gg_share, group, scatter_dimension=0, tiled=True)

    piece = width // dp_count

    def spread_columns(block):
        return lax.all_to_all(
            block.reshape(slot_total, dp_count, piece), "dp", split_axis=1, concat_axis=0, tiled=True
        ).reshape(dp_count * slot_total, piece)

    joined_grads = jnp.concatenate([grad_gate_pre, grad_up_pre], axis=1)
    rows_all = spread_columns(rows_in)
    grads_all = spread_columns(grads_in)
    joined_all = lax.all_gather(joined_grads, "dp", axis=0, tiled=True)
    hidden_all = lax.all_gather(hidden, "dp", axis=0, tiled=True)
    grad_joined = contract_first(rows_all, joined_all)
    grad_down = contract_first(hidden_all, grads_all)
    grad_w_gate = grad_joined[:, :ff_width].astype(jnp.bfloat16)[None]
    grad_w_up = grad_joined[:, ff_width:].astype(jnp.bfloat16)[None]
    grad_w_down = grad_down.astype(jnp.bfloat16)[None]
    return (output, grad_tokens, grad_gates, grad_w_gate, grad_w_up, grad_w_down)


def solution(mesh):
    placed = (
        P(("dp", "outer", "inner"), None),
        P(("dp", "outer", "inner"), None),
        P(("dp", "outer", "inner"), None),
        P(("dp", "outer", "inner"), None),
        P(("outer", "inner"), None, None),
        P(("outer", "inner"), None, None),
        P(("outer", "inner"), None, None),
    )
    return jax.shard_map(
        local,
        mesh=mesh,
        in_specs=placed,
        out_specs=(
            P(("dp", "outer", "inner"), None),
            P(("dp", "outer", "inner"), None),
            P(("dp", "outer", "inner"), None),
            P(("outer", "inner"), "dp", None),
            P(("outer", "inner"), "dp", None),
            P(("outer", "inner"), None, "dp"),
        ),
        check_vma=False,
    )
```

```python
import jax
import jax.numpy as jnp
from jax import lax
from jax.sharding import PartitionSpec as P


def contract_last(left, right):
    return lax.dot_general(
        left, right, (((1,), (1,)), ((), ())), preferred_element_type=jnp.float32
    )


def contract_first(left, right):
    return lax.dot_general(
        left, right, (((0,), (0,)), ((), ())), preferred_element_type=jnp.float32
    )


def expert_rows(rows_in, grads_in, gate_mat, up_mat, down_mat):
    gate_pre = jnp.dot(rows_in, gate_mat, preferred_element_type=jnp.float32)
    up_pre = jnp.dot(rows_in, up_mat, preferred_element_type=jnp.float32)
    sigma = jax.nn.sigmoid(gate_pre)
    silu_value = gate_pre * sigma
    hidden = (silu_value * up_pre).astype(jnp.bfloat16)
    expert_out = jnp.dot(hidden, down_mat, preferred_element_type=jnp.float32).astype(jnp.bfloat16)
    grad_hidden = contract_last(grads_in, down_mat)
    slope = sigma * (1.0 + gate_pre * (1.0 - sigma))
    grad_gate_pre = (grad_hidden * up_pre * slope).astype(jnp.bfloat16)
    grad_up_pre = (grad_hidden * silu_value).astype(jnp.bfloat16)
    pair_grad = (
        contract_last(grad_gate_pre, gate_mat) + contract_last(grad_up_pre, up_mat)
    ).astype(jnp.bfloat16)
    return (hidden, expert_out, grad_gate_pre, grad_up_pre, pair_grad)


def local(tokens, expert_ids, gate_values, upstream, w_gate, w_up, w_down):
    local_tokens = tokens.shape[0]
    width = tokens.shape[1]
    top_count = expert_ids.shape[1]
    ff_width = w_gate.shape[2]
    outer_count = lax.axis_size("outer")
    inner_count = lax.axis_size("inner")
    expert_count = outer_count * inner_count
    capacity = min(local_tokens, 3 * local_tokens * top_count // (2 * expert_count))
    pair_count = local_tokens * top_count
    flat_ids = expert_ids.reshape(-1)
    flat_gates = gate_values.reshape(-1)
    onehot = (flat_ids[:, None] == jnp.arange(expert_count, dtype=jnp.int32)[None, :]).astype(
        jnp.int32
    )
    slot_rank = jnp.sum((jnp.cumsum(onehot, axis=0) - onehot) * onehot, axis=1)
    pair_slot = flat_ids * capacity + slot_rank
    slot_pair = (
        jnp.full((expert_count * capacity,), pair_count, jnp.int32)
        .at[pair_slot]
        .set(jnp.arange(pair_count, dtype=jnp.int32))
    )
    slot_token = jnp.where(slot_pair < pair_count, slot_pair // top_count, local_tokens)
    token_pad = jnp.concatenate([tokens, jnp.zeros((1, width), jnp.bfloat16)], axis=0)
    upstream_pad = jnp.concatenate([upstream, jnp.zeros((1, width), jnp.bfloat16)], axis=0)
    gate_pad = jnp.concatenate([flat_gates, jnp.zeros((1,), jnp.float32)], axis=0)
    send_rows = token_pad[slot_token]
    send_grads = (
        gate_pad[slot_pair][:, None] * upstream_pad[slot_token].astype(jnp.float32)
    ).astype(jnp.bfloat16)
    flat_shape = (expert_count, capacity, 2 * width)
    got = lax.all_to_all(
        jnp.concatenate([send_rows, send_grads], axis=1).reshape(flat_shape),
        ("outer", "inner"),
        split_axis=0,
        concat_axis=0,
        tiled=True,
    ).reshape(-1, 2 * width)
    rows_in = got[:, :width]
    grads_in = got[:, width:]
    hidden, expert_out, grad_gate_pre, grad_up_pre, pair_grad = expert_rows(
        rows_in, grads_in, w_gate[0], w_up[0], w_down[0]
    )
    back = lax.all_to_all(
        jnp.concatenate([expert_out, pair_grad], axis=1).reshape(flat_shape),
        ("outer", "inner"),
        split_axis=0,
        concat_axis=0,
        tiled=True,
    ).reshape(-1, 2 * width)
    dp_count = lax.axis_size("dp")
    slot_total = rows_in.shape[0]
    piece = width // dp_count

    joined_grads = jnp.concatenate([grad_gate_pre, grad_up_pre], axis=1)
    both_all = lax.all_to_all(
        got.reshape(slot_total, 2, dp_count, piece).transpose(0, 2, 1, 3),
        "dp",
        split_axis=1,
        concat_axis=0,
        tiled=True,
    ).reshape(dp_count * slot_total, 2, piece)
    rows_all = both_all[:, 0]
    grads_all = both_all[:, 1]
    joined_all = lax.all_gather(joined_grads, "dp", axis=0, tiled=True)
    hidden_all = lax.all_gather(hidden, "dp", axis=0, tiled=True)
    grad_joined = contract_first(rows_all, joined_all)
    grad_down = contract_first(hidden_all, grads_all)
    pair_both = back[pair_slot]
    pair_out = pair_both[:, :width].reshape(local_tokens, top_count, width)
    pair_back = pair_both[:, width:].reshape(local_tokens, top_count, width)
    output = jnp.sum(gate_values[:, :, None] * pair_out.astype(jnp.float32), axis=1).astype(
        jnp.bfloat16
    )
    grad_tokens = jnp.sum(pair_back.astype(jnp.float32), axis=1).astype(jnp.bfloat16)
    grad_gates = jnp.einsum("tkd,td->tk", pair_out, upstream, preferred_element_type=jnp.float32)
    grad_w_gate = grad_joined[:, :ff_width].astype(jnp.bfloat16)[None]
    grad_w_up = grad_joined[:, ff_width:].astype(jnp.bfloat16)[None]
    grad_w_down = grad_down.astype(jnp.bfloat16)[None]
    return (output, grad_tokens, grad_gates, grad_w_gate, grad_w_up, grad_w_down)


def solution(mesh):
    placed = (
        P(("dp", "outer", "inner"), None),
        P(("dp", "outer", "inner"), None),
        P(("dp", "outer", "inner"), None),
        P(("dp", "outer", "inner"), None),
        P(("outer", "inner"), None, None),
        P(("outer", "inner"), None, None),
        P(("outer", "inner"), None, None),
    )
    return jax.shard_map(
        local,
        mesh=mesh,
        in_specs=placed,
        out_specs=(
            P(("dp", "outer", "inner"), None),
            P(("dp", "outer", "inner"), None),
            P(("dp", "outer", "inner"), None),
            P(("outer", "inner"), "dp", None),
            P(("outer", "inner"), "dp", None),
            P(("outer", "inner"), None, "dp"),
        ),
        check_vma=False,
    )
```

```python
import jax
import jax.numpy as jnp
from jax import lax
from jax.sharding import PartitionSpec as P


def contract_last(left, right):
    return lax.dot_general(
        left, right, (((1,), (1,)), ((), ())), preferred_element_type=jnp.float32
    )


def contract_first(left, right):
    return lax.dot_general(
        left, right, (((0,), (0,)), ((), ())), preferred_element_type=jnp.float32
    )


def expert_rows(rows_in, grads_in, gate_mat, up_mat, down_mat):
    gate_pre = jnp.dot(rows_in, gate_mat, preferred_element_type=jnp.float32)
    up_pre = jnp.dot(rows_in, up_mat, preferred_element_type=jnp.float32)
    sigma = jax.nn.sigmoid(gate_pre)
    silu_value = gate_pre * sigma
    hidden = (silu_value * up_pre).astype(jnp.bfloat16)
    expert_out = jnp.dot(hidden, down_mat, preferred_element_type=jnp.float32).astype(jnp.bfloat16)
    grad_hidden = contract_last(grads_in, down_mat)
    slope = sigma * (1.0 + gate_pre * (1.0 - sigma))
    grad_gate_pre = (grad_hidden * up_pre * slope).astype(jnp.bfloat16)
    grad_up_pre = (grad_hidden * silu_value).astype(jnp.bfloat16)
    pair_grad = (
        contract_last(grad_gate_pre, gate_mat) + contract_last(grad_up_pre, up_mat)
    ).astype(jnp.bfloat16)
    return (hidden, expert_out, grad_gate_pre, grad_up_pre, pair_grad)


def local(tokens, expert_ids, gate_values, upstream, w_gate, w_up, w_down):
    local_tokens = tokens.shape[0]
    width = tokens.shape[1]
    top_count = expert_ids.shape[1]
    ff_width = w_gate.shape[2]
    outer_count = lax.axis_size("outer")
    inner_count = lax.axis_size("inner")
    expert_count = outer_count * inner_count
    capacity = min(local_tokens, 3 * local_tokens * top_count // (2 * expert_count))
    pair_count = local_tokens * top_count
    flat_ids = expert_ids.reshape(-1)
    flat_gates = gate_values.reshape(-1)
    onehot = (flat_ids[:, None] == jnp.arange(expert_count, dtype=jnp.int32)[None, :]).astype(
        jnp.int32
    )
    slot_rank = jnp.sum((jnp.cumsum(onehot, axis=0) - onehot) * onehot, axis=1)
    pair_slot = flat_ids * capacity + slot_rank
    slot_pair = (
        jnp.full((expert_count * capacity,), pair_count, jnp.int32)
        .at[pair_slot]
        .set(jnp.arange(pair_count, dtype=jnp.int32))
    )
    slot_token = jnp.where(slot_pair < pair_count, slot_pair // top_count, local_tokens)
    token_pad = jnp.concatenate([tokens, jnp.zeros((1, width), jnp.bfloat16)], axis=0)
    upstream_pad = jnp.concatenate([upstream, jnp.zeros((1, width), jnp.bfloat16)], axis=0)
    gate_pad = jnp.concatenate([flat_gates, jnp.zeros((1,), jnp.float32)], axis=0)
    send_rows = token_pad[slot_token]
    send_grads = (
        gate_pad[slot_pair][:, None] * upstream_pad[slot_token].astype(jnp.float32)
    ).astype(jnp.bfloat16)
    flat_shape = (expert_count, capacity, width)
    got_rows, got_grads = (
        lax.all_to_all(
            send_rows.reshape(flat_shape),
            ("outer", "inner"),
            split_axis=0,
            concat_axis=0,
            tiled=True,
        ),
        lax.all_to_all(
            send_grads.reshape(flat_shape),
            ("outer", "inner"),
            split_axis=0,
            concat_axis=0,
            tiled=True,
        ),
    )
    rows_in = got_rows.reshape(-1, width)
    grads_in = got_grads.reshape(-1, width)
    hidden, expert_out, grad_gate_pre, grad_up_pre, pair_grad = expert_rows(
        rows_in, grads_in, w_gate[0], w_up[0], w_down[0]
    )
    back_out, back_grad = (
        lax.all_to_all(
            expert_out.reshape(flat_shape),
            ("outer", "inner"),
            split_axis=0,
            concat_axis=0,
            tiled=True,
        ),
        lax.all_to_all(
            pair_grad.reshape(flat_shape),
            ("outer", "inner"),
            split_axis=0,
            concat_axis=0,
            tiled=True,
        ),
    )
    dp_count = lax.axis_size("dp")
    dp_index = lax.axis_index("dp")
    slot_total = rows_in.shape[0]
    piece = width // dp_count
    both_in = jnp.concatenate(
        [rows_in.reshape(slot_total, dp_count, piece), grads_in.reshape(slot_total, dp_count, piece)], axis=2
    )
    pieces = [lax.dynamic_index_in_dim(both_in, dp_index, axis=1, keepdims=False)]
    for shift in range(1, dp_count):
        outgoing = lax.dynamic_index_in_dim(both_in, (dp_index + shift) % dp_count, axis=1, keepdims=False)
        pieces.append(
            lax.ppermute(outgoing, "dp", [(j, (j + shift) % dp_count) for j in range(dp_count)])
        )
    both_all = jnp.concatenate(pieces, axis=0)
    source_order = (dp_index - jnp.arange(dp_count)) % dp_count
    joined_grads = jnp.concatenate([grad_gate_pre, grad_up_pre], axis=1)
    joined_all = jnp.take(
        lax.all_gather(joined_grads, "dp", axis=0, tiled=False), source_order, axis=0
    ).reshape(dp_count * slot_total, -1)
    hidden_all = jnp.take(
        lax.all_gather(hidden, "dp", axis=0, tiled=False), source_order, axis=0
    ).reshape(dp_count * slot_total, -1)
    grad_joined = contract_first(both_all[:, :piece], joined_all)
    grad_down = contract_first(hidden_all, both_all[:, piece:])
    pair_out = back_out.reshape(-1, width)[pair_slot].reshape(local_tokens, top_count, width)
    pair_back = back_grad.reshape(-1, width)[pair_slot].reshape(local_tokens, top_count, width)
    output = jnp.sum(gate_values[:, :, None] * pair_out.astype(jnp.float32), axis=1).astype(
        jnp.bfloat16
    )
    grad_tokens = jnp.sum(pair_back.astype(jnp.float32), axis=1).astype(jnp.bfloat16)
    grad_gates = jnp.einsum("tkd,td->tk", pair_out, upstream, preferred_element_type=jnp.float32)
    grad_w_gate = grad_joined[:, :ff_width].astype(jnp.bfloat16)[None]
    grad_w_up = grad_joined[:, ff_width:].astype(jnp.bfloat16)[None]
    grad_w_down = grad_down.astype(jnp.bfloat16)[None]
    return (output, grad_tokens, grad_gates, grad_w_gate, grad_w_up, grad_w_down)


def solution(mesh):
    placed = (
        P(("dp", "outer", "inner"), None),
        P(("dp", "outer", "inner"), None),
        P(("dp", "outer", "inner"), None),
        P(("dp", "outer", "inner"), None),
        P(("outer", "inner"), None, None),
        P(("outer", "inner"), None, None),
        P(("outer", "inner"), None, None),
    )
    return jax.shard_map(
        local,
        mesh=mesh,
        in_specs=placed,
        out_specs=(
            P(("dp", "outer", "inner"), None),
            P(("dp", "outer", "inner"), None),
            P(("dp", "outer", "inner"), None),
            P(("outer", "inner"), "dp", None),
            P(("outer", "inner"), "dp", None),
            P(("outer", "inner"), None, "dp"),
        ),
        check_vma=False,
    )
```

```python
import jax
import jax.numpy as jnp
from jax import lax
from jax.sharding import PartitionSpec as P


def contract_last(left, right):
    return lax.dot_general(
        left, right, (((1,), (1,)), ((), ())), preferred_element_type=jnp.float32
    )


def contract_first(left, right):
    return lax.dot_general(
        left, right, (((0,), (0,)), ((), ())), preferred_element_type=jnp.float32
    )


def expert_rows(rows_in, grads_in, gate_mat, up_mat, down_mat):
    gate_pre = jnp.dot(rows_in, gate_mat, preferred_element_type=jnp.float32)
    up_pre = jnp.dot(rows_in, up_mat, preferred_element_type=jnp.float32)
    sigma = jax.nn.sigmoid(gate_pre)
    silu_value = gate_pre * sigma
    hidden = (silu_value * up_pre).astype(jnp.bfloat16)
    expert_out = jnp.dot(hidden, down_mat, preferred_element_type=jnp.float32).astype(jnp.bfloat16)
    grad_hidden = contract_last(grads_in, down_mat)
    slope = sigma * (1.0 + gate_pre * (1.0 - sigma))
    grad_gate_pre = (grad_hidden * up_pre * slope).astype(jnp.bfloat16)
    grad_up_pre = (grad_hidden * silu_value).astype(jnp.bfloat16)
    pair_grad = (
        contract_last(grad_gate_pre, gate_mat) + contract_last(grad_up_pre, up_mat)
    ).astype(jnp.bfloat16)
    return (hidden, expert_out, grad_gate_pre, grad_up_pre, pair_grad)


def local(tokens, expert_ids, gate_values, upstream, w_gate, w_up, w_down):
    local_tokens = tokens.shape[0]
    width = tokens.shape[1]
    top_count = expert_ids.shape[1]
    ff_width = w_gate.shape[2]
    outer_count = lax.axis_size("outer")
    inner_count = lax.axis_size("inner")
    expert_count = outer_count * inner_count
    capacity = min(local_tokens, 3 * local_tokens * top_count // (2 * expert_count))
    pair_count = local_tokens * top_count
    flat_ids = expert_ids.reshape(-1)
    flat_gates = gate_values.reshape(-1)
    onehot = (flat_ids[:, None] == jnp.arange(expert_count, dtype=jnp.int32)[None, :]).astype(
        jnp.int32
    )
    slot_rank = jnp.sum((jnp.cumsum(onehot, axis=0) - onehot) * onehot, axis=1)
    pair_slot = flat_ids * capacity + slot_rank
    slot_pair = (
        jnp.full((expert_count * capacity,), pair_count, jnp.int32)
        .at[pair_slot]
        .set(jnp.arange(pair_count, dtype=jnp.int32))
    )
    slot_token = jnp.where(slot_pair < pair_count, slot_pair // top_count, local_tokens)
    token_pad = jnp.concatenate([tokens, jnp.zeros((1, width), jnp.bfloat16)], axis=0)
    upstream_pad = jnp.concatenate([upstream, jnp.zeros((1, width), jnp.bfloat16)], axis=0)
    gate_pad = jnp.concatenate([flat_gates, jnp.zeros((1,), jnp.float32)], axis=0)
    send_rows = token_pad[slot_token]
    send_grads = (
        gate_pad[slot_pair][:, None] * upstream_pad[slot_token].astype(jnp.float32)
    ).astype(jnp.bfloat16)
    flat_shape = (expert_count, capacity, width)
    got_rows, got_grads = (
        lax.all_to_all(
            send_rows.reshape(flat_shape),
            ("outer", "inner"),
            split_axis=0,
            concat_axis=0,
            tiled=True,
        ),
        lax.all_to_all(
            send_grads.reshape(flat_shape),
            ("outer", "inner"),
            split_axis=0,
            concat_axis=0,
            tiled=True,
        ),
    )
    rows_in = got_rows.reshape(-1, width)
    grads_in = got_grads.reshape(-1, width)
    hidden, expert_out, grad_gate_pre, grad_up_pre, pair_grad = expert_rows(
        rows_in, grads_in, w_gate[0], w_up[0], w_down[0]
    )
    back_out, back_grad = (
        lax.all_to_all(
            expert_out.reshape(flat_shape),
            ("outer", "inner"),
            split_axis=0,
            concat_axis=0,
            tiled=True,
        ),
        lax.all_to_all(
            pair_grad.reshape(flat_shape),
            ("outer", "inner"),
            split_axis=0,
            concat_axis=0,
            tiled=True,
        ),
    )
    dp_count = lax.axis_size("dp")
    piece = width // dp_count
    column_pieces = jnp.stack(
        [rows_in[:, part * piece:(part + 1) * piece] for part in range(dp_count)], axis=0
    )
    rows_all = lax.all_to_all(column_pieces, "dp", split_axis=0, concat_axis=0, tiled=True)
    joined_grads = jnp.concatenate([grad_gate_pre, grad_up_pre], axis=1)
    joined_all = lax.all_gather(joined_grads, "dp", axis=0, tiled=False)
    grad_joined = lax.dot_general(
        rows_all, joined_all, (((0, 1), (0, 1)), ((), ())), preferred_element_type=jnp.float32
    )
    columns = grads_in
    grad_down = (
        lax.psum_scatter(
            contract_first(columns, hidden).astype(jnp.bfloat16),
            "dp",
            scatter_dimension=0,
            tiled=True,
        )
        .astype(jnp.float32)
        .T
    )
    pair_out = back_out.reshape(-1, width)[pair_slot].reshape(local_tokens, top_count, width)
    pair_back = back_grad.reshape(-1, width)[pair_slot].reshape(local_tokens, top_count, width)
    output = jnp.sum(gate_values[:, :, None] * pair_out.astype(jnp.float32), axis=1).astype(
        jnp.bfloat16
    )
    grad_tokens = jnp.sum(pair_back.astype(jnp.float32), axis=1).astype(jnp.bfloat16)
    grad_gates = jnp.einsum("tkd,td->tk", pair_out, upstream, preferred_element_type=jnp.float32)
    grad_w_gate = grad_joined[:, :ff_width].astype(jnp.bfloat16)[None]
    grad_w_up = grad_joined[:, ff_width:].astype(jnp.bfloat16)[None]
    grad_w_down = grad_down.astype(jnp.bfloat16)[None]
    return (output, grad_tokens, grad_gates, grad_w_gate, grad_w_up, grad_w_down)


def solution(mesh):
    placed = (
        P(("dp", "outer", "inner"), None),
        P(("dp", "outer", "inner"), None),
        P(("dp", "outer", "inner"), None),
        P(("dp", "outer", "inner"), None),
        P(("outer", "inner"), None, None),
        P(("outer", "inner"), None, None),
        P(("outer", "inner"), None, None),
    )
    return jax.shard_map(
        local,
        mesh=mesh,
        in_specs=placed,
        out_specs=(
            P(("dp", "outer", "inner"), None),
            P(("dp", "outer", "inner"), None),
            P(("dp", "outer", "inner"), None),
            P(("outer", "inner"), "dp", None),
            P(("outer", "inner"), "dp", None),
            P(("outer", "inner"), None, "dp"),
        ),
        check_vma=False,
    )
```

```python
import jax
import jax.numpy as jnp
from jax import lax
from jax.sharding import PartitionSpec as P


def contract_last(left, right):
    return lax.dot_general(
        left, right, (((1,), (1,)), ((), ())), preferred_element_type=jnp.float32
    )


def contract_first(left, right):
    return lax.dot_general(
        left, right, (((0,), (0,)), ((), ())), preferred_element_type=jnp.float32
    )


def expert_rows(rows_in, grads_in, gate_mat, up_mat, down_mat):
    gate_pre = jnp.dot(rows_in, gate_mat, preferred_element_type=jnp.float32)
    up_pre = jnp.dot(rows_in, up_mat, preferred_element_type=jnp.float32)
    sigma = jax.nn.sigmoid(gate_pre)
    silu_value = gate_pre * sigma
    hidden = (silu_value * up_pre).astype(jnp.bfloat16)
    expert_out = jnp.dot(hidden, down_mat, preferred_element_type=jnp.float32).astype(jnp.bfloat16)
    grad_hidden = contract_last(grads_in, down_mat)
    slope = sigma * (1.0 + gate_pre * (1.0 - sigma))
    grad_gate_pre = (grad_hidden * up_pre * slope).astype(jnp.bfloat16)
    grad_up_pre = (grad_hidden * silu_value).astype(jnp.bfloat16)
    pair_grad = (
        contract_last(grad_gate_pre, gate_mat) + contract_last(grad_up_pre, up_mat)
    ).astype(jnp.bfloat16)
    return (hidden, expert_out, grad_gate_pre, grad_up_pre, pair_grad)


def local(tokens, expert_ids, gate_values, upstream, w_gate, w_up, w_down):
    local_tokens = tokens.shape[0]
    width = tokens.shape[1]
    top_count = expert_ids.shape[1]
    ff_width = w_gate.shape[2]
    outer_count = lax.axis_size("outer")
    inner_count = lax.axis_size("inner")
    expert_count = outer_count * inner_count
    capacity = min(local_tokens, 3 * local_tokens * top_count // (2 * expert_count))
    pair_count = local_tokens * top_count
    flat_ids = expert_ids.reshape(-1)
    flat_gates = gate_values.reshape(-1)
    onehot = (flat_ids[:, None] == jnp.arange(expert_count, dtype=jnp.int32)[None, :]).astype(
        jnp.int32
    )
    slot_rank = jnp.sum((jnp.cumsum(onehot, axis=0) - onehot) * onehot, axis=1)
    pair_slot = flat_ids * capacity + slot_rank
    slot_pair = (
        jnp.full((expert_count * capacity,), pair_count, jnp.int32)
        .at[pair_slot]
        .set(jnp.arange(pair_count, dtype=jnp.int32))
    )
    slot_token = jnp.where(slot_pair < pair_count, slot_pair // top_count, local_tokens)
    token_pad = jnp.concatenate([tokens, jnp.zeros((1, width), jnp.bfloat16)], axis=0)
    upstream_pad = jnp.concatenate([upstream, jnp.zeros((1, width), jnp.bfloat16)], axis=0)
    gate_pad = jnp.concatenate([flat_gates, jnp.zeros((1,), jnp.float32)], axis=0)
    send_rows = token_pad[slot_token]
    send_grads = (
        gate_pad[slot_pair][:, None] * upstream_pad[slot_token].astype(jnp.float32)
    ).astype(jnp.bfloat16)
    fold = 1
    while (capacity * fold) % 16 or (width // fold) % 128 or width % fold:
        fold += 1
    if (width // fold) % 128 or width % fold:
        fold = 1
    flat_shape = (expert_count, capacity * fold, width // fold)
    got_rows, got_grads = (
        lax.all_to_all(
            send_rows.reshape(flat_shape),
            ("outer", "inner"),
            split_axis=0,
            concat_axis=0,
            tiled=True,
        ),
        lax.all_to_all(
            send_grads.reshape(flat_shape),
            ("outer", "inner"),
            split_axis=0,
            concat_axis=0,
            tiled=True,
        ),
    )
    rows_in = got_rows.reshape(-1, width)
    grads_in = got_grads.reshape(-1, width)
    hidden, expert_out, grad_gate_pre, grad_up_pre, pair_grad = expert_rows(
        rows_in, grads_in, w_gate[0], w_up[0], w_down[0]
    )
    dp_count = lax.axis_size("dp")
    piece = width // dp_count
    rows_all = lax.all_to_all(
        jnp.stack([rows_in[:, part * piece:(part + 1) * piece] for part in range(dp_count)], axis=0),
        "dp",
        split_axis=0,
        concat_axis=0,
        tiled=True,
    )
    expert_out, pair_grad, rows_all = lax.optimization_barrier((expert_out, pair_grad, rows_all))
    back_out, back_grad = (
        lax.all_to_all(
            expert_out.reshape(flat_shape),
            ("outer", "inner"),
            split_axis=0,
            concat_axis=0,
            tiled=True,
        ),
        lax.all_to_all(
            pair_grad.reshape(flat_shape),
            ("outer", "inner"),
            split_axis=0,
            concat_axis=0,
            tiled=True,
        ),
    )
    joined_grads = jnp.concatenate([grad_gate_pre, grad_up_pre], axis=1)
    joined_all = lax.all_gather(joined_grads, "dp", axis=0, tiled=False)
    grad_joined = lax.dot_general(
        rows_all, joined_all, (((0, 1), (0, 1)), ((), ())), preferred_element_type=jnp.float32
    )
    columns = grads_in
    grad_down = (
        lax.psum_scatter(
            contract_first(columns, hidden).astype(jnp.bfloat16),
            "dp",
            scatter_dimension=0,
            tiled=True,
        )
        .astype(jnp.float32)
        .T
    )
    pair_out = back_out.reshape(-1, width)[pair_slot].reshape(local_tokens, top_count, width)
    pair_back = back_grad.reshape(-1, width)[pair_slot].reshape(local_tokens, top_count, width)
    output = jnp.sum(gate_values[:, :, None] * pair_out.astype(jnp.float32), axis=1).astype(
        jnp.bfloat16
    )
    grad_tokens = jnp.sum(pair_back.astype(jnp.float32), axis=1).astype(jnp.bfloat16)
    grad_gates = jnp.einsum("tkd,td->tk", pair_out, upstream, preferred_element_type=jnp.float32)
    grad_w_gate = grad_joined[:, :ff_width].astype(jnp.bfloat16)[None]
    grad_w_up = grad_joined[:, ff_width:].astype(jnp.bfloat16)[None]
    grad_w_down = grad_down.astype(jnp.bfloat16)[None]
    return (output, grad_tokens, grad_gates, grad_w_gate, grad_w_up, grad_w_down)


def solution(mesh):
    placed = (
        P(("dp", "outer", "inner"), None),
        P(("dp", "outer", "inner"), None),
        P(("dp", "outer", "inner"), None),
        P(("dp", "outer", "inner"), None),
        P(("outer", "inner"), None, None),
        P(("outer", "inner"), None, None),
        P(("outer", "inner"), None, None),
    )
    return jax.shard_map(
        local,
        mesh=mesh,
        in_specs=placed,
        out_specs=(
            P(("dp", "outer", "inner"), None),
            P(("dp", "outer", "inner"), None),
            P(("dp", "outer", "inner"), None),
            P(("outer", "inner"), "dp", None),
            P(("outer", "inner"), "dp", None),
            P(("outer", "inner"), None, "dp"),
        ),
        check_vma=False,
    )
```

```python
import jax
import jax.numpy as jnp
from jax import lax
from jax.sharding import PartitionSpec as P


def contract_last(left, right):
    return lax.dot_general(
        left, right, (((1,), (1,)), ((), ())), preferred_element_type=jnp.float32
    )


def contract_first(left, right):
    return lax.dot_general(
        left, right, (((0,), (0,)), ((), ())), preferred_element_type=jnp.float32
    )


def expert_rows(rows_in, grads_in, gate_mat, up_mat, down_mat):
    gate_pre = jnp.dot(rows_in, gate_mat, preferred_element_type=jnp.float32)
    up_pre = jnp.dot(rows_in, up_mat, preferred_element_type=jnp.float32)
    sigma = jax.nn.sigmoid(gate_pre)
    silu_value = gate_pre * sigma
    hidden = (silu_value * up_pre).astype(jnp.bfloat16)
    expert_out = jnp.dot(hidden, down_mat, preferred_element_type=jnp.float32).astype(jnp.bfloat16)
    grad_hidden = contract_last(grads_in, down_mat)
    slope = sigma * (1.0 + gate_pre * (1.0 - sigma))
    grad_gate_pre = (grad_hidden * up_pre * slope).astype(jnp.bfloat16)
    grad_up_pre = (grad_hidden * silu_value).astype(jnp.bfloat16)
    pair_grad = (
        contract_last(grad_gate_pre, gate_mat) + contract_last(grad_up_pre, up_mat)
    ).astype(jnp.bfloat16)
    return (hidden, expert_out, grad_gate_pre, grad_up_pre, pair_grad)


def local(tokens, expert_ids, gate_values, upstream, w_gate, w_up, w_down):
    local_tokens = tokens.shape[0]
    width = tokens.shape[1]
    top_count = expert_ids.shape[1]
    ff_width = w_gate.shape[2]
    outer_count = lax.axis_size("outer")
    inner_count = lax.axis_size("inner")
    expert_count = outer_count * inner_count
    capacity = min(local_tokens, 3 * local_tokens * top_count // (2 * expert_count))
    pair_count = local_tokens * top_count
    flat_ids = expert_ids.reshape(-1)
    flat_gates = gate_values.reshape(-1)
    onehot = (flat_ids[:, None] == jnp.arange(expert_count, dtype=jnp.int32)[None, :]).astype(
        jnp.int32
    )
    slot_rank = jnp.sum((jnp.cumsum(onehot, axis=0) - onehot) * onehot, axis=1)
    pair_slot = flat_ids * capacity + slot_rank
    slot_pair = (
        jnp.full((expert_count * capacity,), pair_count, jnp.int32)
        .at[pair_slot]
        .set(jnp.arange(pair_count, dtype=jnp.int32))
    )
    slot_token = jnp.where(slot_pair < pair_count, slot_pair // top_count, local_tokens)
    token_pad = jnp.concatenate([tokens, jnp.zeros((1, width), jnp.bfloat16)], axis=0)
    upstream_pad = jnp.concatenate([upstream, jnp.zeros((1, width), jnp.bfloat16)], axis=0)
    gate_pad = jnp.concatenate([flat_gates, jnp.zeros((1,), jnp.float32)], axis=0)
    send_rows = token_pad[slot_token]
    send_grads = (
        gate_pad[slot_pair][:, None] * upstream_pad[slot_token].astype(jnp.float32)
    ).astype(jnp.bfloat16)
    fold = 1
    while (capacity * fold) % 16 or (width // fold) % 128 or width % fold:
        fold += 1
    if (width // fold) % 128 or width % fold:
        fold = 1
    flat_shape = (expert_count, capacity * fold, width // fold)
    got_rows, got_grads = (
        lax.all_to_all(
            send_rows.reshape(flat_shape),
            ("outer", "inner"),
            split_axis=0,
            concat_axis=0,
            tiled=True,
        ),
        lax.all_to_all(
            send_grads.reshape(flat_shape),
            ("outer", "inner"),
            split_axis=0,
            concat_axis=0,
            tiled=True,
        ),
    )
    rows_in = got_rows.reshape(-1, width)
    grads_in = got_grads.reshape(-1, width)
    dp_count = lax.axis_size("dp")
    piece = width // dp_count
    rows_all = lax.all_to_all(
        jnp.stack([rows_in[:, part * piece:(part + 1) * piece] for part in range(dp_count)], axis=0),
        "dp",
        split_axis=0,
        concat_axis=0,
        tiled=True,
    )
    gate_mat, up_mat, down_mat = w_gate[0], w_up[0], w_down[0]
    gate_pre = jnp.dot(rows_in, gate_mat, preferred_element_type=jnp.float32)
    up_pre = jnp.dot(rows_in, up_mat, preferred_element_type=jnp.float32)
    sigma = jax.nn.sigmoid(gate_pre)
    silu_value = gate_pre * sigma
    hidden = (silu_value * up_pre).astype(jnp.bfloat16)
    expert_out = jnp.dot(hidden, down_mat, preferred_element_type=jnp.float32).astype(jnp.bfloat16)
    grads_in, rows_all = lax.optimization_barrier((grads_in, rows_all))
    grad_hidden = contract_last(grads_in, down_mat)
    slope = sigma * (1.0 + gate_pre * (1.0 - sigma))
    grad_gate_pre = (grad_hidden * up_pre * slope).astype(jnp.bfloat16)
    grad_up_pre = (grad_hidden * silu_value).astype(jnp.bfloat16)
    pair_grad = (
        contract_last(grad_gate_pre, gate_mat) + contract_last(grad_up_pre, up_mat)
    ).astype(jnp.bfloat16)
    back_out, back_grad = (
        lax.all_to_all(
            expert_out.reshape(flat_shape),
            ("outer", "inner"),
            split_axis=0,
            concat_axis=0,
            tiled=True,
        ),
        lax.all_to_all(
            pair_grad.reshape(flat_shape),
            ("outer", "inner"),
            split_axis=0,
            concat_axis=0,
            tiled=True,
        ),
    )
    joined_grads = jnp.concatenate([grad_gate_pre, grad_up_pre], axis=1)
    joined_all = lax.all_gather(joined_grads, "dp", axis=0, tiled=False)
    grad_joined = lax.dot_general(
        rows_all, joined_all, (((0, 1), (0, 1)), ((), ())), preferred_element_type=jnp.float32
    )
    columns = grads_in
    grad_down = (
        lax.psum_scatter(
            contract_first(columns, hidden).astype(jnp.bfloat16),
            "dp",
            scatter_dimension=0,
            tiled=True,
        )
        .astype(jnp.float32)
        .T
    )
    pair_out = back_out.reshape(-1, width)[pair_slot].reshape(local_tokens, top_count, width)
    pair_back = back_grad.reshape(-1, width)[pair_slot].reshape(local_tokens, top_count, width)
    output = jnp.sum(gate_values[:, :, None] * pair_out.astype(jnp.float32), axis=1).astype(
        jnp.bfloat16
    )
    grad_tokens = jnp.sum(pair_back.astype(jnp.float32), axis=1).astype(jnp.bfloat16)
    grad_gates = jnp.einsum("tkd,td->tk", pair_out, upstream, preferred_element_type=jnp.float32)
    grad_w_gate = grad_joined[:, :ff_width].astype(jnp.bfloat16)[None]
    grad_w_up = grad_joined[:, ff_width:].astype(jnp.bfloat16)[None]
    grad_w_down = grad_down.astype(jnp.bfloat16)[None]
    return (output, grad_tokens, grad_gates, grad_w_gate, grad_w_up, grad_w_down)


def solution(mesh):
    placed = (
        P(("dp", "outer", "inner"), None),
        P(("dp", "outer", "inner"), None),
        P(("dp", "outer", "inner"), None),
        P(("dp", "outer", "inner"), None),
        P(("outer", "inner"), None, None),
        P(("outer", "inner"), None, None),
        P(("outer", "inner"), None, None),
    )
    return jax.shard_map(
        local,
        mesh=mesh,
        in_specs=placed,
        out_specs=(
            P(("dp", "outer", "inner"), None),
            P(("dp", "outer", "inner"), None),
            P(("dp", "outer", "inner"), None),
            P(("outer", "inner"), "dp", None),
            P(("outer", "inner"), "dp", None),
            P(("outer", "inner"), None, "dp"),
        ),
        check_vma=False,
    )
```

```python
import jax
import jax.numpy as jnp
from jax import lax
from jax.sharding import PartitionSpec as P


def contract_last(left, right):
    return lax.dot_general(
        left, right, (((1,), (1,)), ((), ())), preferred_element_type=jnp.float32
    )


def contract_first(left, right):
    return lax.dot_general(
        left, right, (((0,), (0,)), ((), ())), preferred_element_type=jnp.float32
    )


def expert_rows(rows_in, grads_in, gate_mat, up_mat, down_mat):
    gate_pre = jnp.dot(rows_in, gate_mat, preferred_element_type=jnp.float32)
    up_pre = jnp.dot(rows_in, up_mat, preferred_element_type=jnp.float32)
    sigma = jax.nn.sigmoid(gate_pre)
    silu_value = gate_pre * sigma
    hidden = (silu_value * up_pre).astype(jnp.bfloat16)
    expert_out = jnp.dot(hidden, down_mat, preferred_element_type=jnp.float32).astype(jnp.bfloat16)
    grad_hidden = contract_last(grads_in, down_mat)
    slope = sigma * (1.0 + gate_pre * (1.0 - sigma))
    grad_gate_pre = (grad_hidden * up_pre * slope).astype(jnp.bfloat16)
    grad_up_pre = (grad_hidden * silu_value).astype(jnp.bfloat16)
    pair_grad = (
        contract_last(grad_gate_pre, gate_mat) + contract_last(grad_up_pre, up_mat)
    ).astype(jnp.bfloat16)
    return (hidden, expert_out, grad_gate_pre, grad_up_pre, pair_grad)


def local(tokens, expert_ids, gate_values, upstream, w_gate, w_up, w_down):
    local_tokens = tokens.shape[0]
    width = tokens.shape[1]
    top_count = expert_ids.shape[1]
    ff_width = w_gate.shape[2]
    outer_count = lax.axis_size("outer")
    inner_count = lax.axis_size("inner")
    expert_count = outer_count * inner_count
    capacity = min(local_tokens, 3 * local_tokens * top_count // (2 * expert_count))
    pair_count = local_tokens * top_count
    flat_ids = expert_ids.reshape(-1)
    flat_gates = gate_values.reshape(-1)
    onehot = (flat_ids[:, None] == jnp.arange(expert_count, dtype=jnp.int32)[None, :]).astype(
        jnp.int32
    )
    slot_rank = jnp.sum((jnp.cumsum(onehot, axis=0) - onehot) * onehot, axis=1)
    pair_slot = flat_ids * capacity + slot_rank
    slot_pair = (
        jnp.full((expert_count * capacity,), pair_count, jnp.int32)
        .at[pair_slot]
        .set(jnp.arange(pair_count, dtype=jnp.int32))
    )
    slot_token = jnp.where(slot_pair < pair_count, slot_pair // top_count, local_tokens)
    token_pad = jnp.concatenate([tokens, jnp.zeros((1, width), jnp.bfloat16)], axis=0)
    upstream_pad = jnp.concatenate([upstream, jnp.zeros((1, width), jnp.bfloat16)], axis=0)
    gate_pad = jnp.concatenate([flat_gates, jnp.zeros((1,), jnp.float32)], axis=0)
    send_rows = token_pad[slot_token]
    send_grads = (
        gate_pad[slot_pair][:, None] * upstream_pad[slot_token].astype(jnp.float32)
    ).astype(jnp.bfloat16)
    fold = 1
    while (capacity * fold) % 16 or (width // fold) % 128 or width % fold:
        fold += 1
    if (width // fold) % 128 or width % fold:
        fold = 1
    flat_shape = (expert_count, capacity * fold, width // fold)
    got_rows, got_grads = (
        lax.all_to_all(
            send_rows.reshape(flat_shape),
            ("outer", "inner"),
            split_axis=0,
            concat_axis=0,
            tiled=True,
        ),
        lax.all_to_all(
            send_grads.reshape(flat_shape),
            ("outer", "inner"),
            split_axis=0,
            concat_axis=0,
            tiled=True,
        ),
    )
    rows_in = got_rows.reshape(-1, width)
    grads_in = got_grads.reshape(-1, width)
    dp_count = lax.axis_size("dp")
    piece = width // dp_count
    dp_index = lax.axis_index("dp")
    arrived = [lax.dynamic_slice_in_dim(rows_in, dp_index * piece, piece, axis=1)]
    for shift in range(1, dp_count):
        outgoing = lax.dynamic_slice_in_dim(rows_in, ((dp_index + shift) % dp_count) * piece, piece, axis=1)
        arrived.append(lax.ppermute(outgoing, "dp", [(j, (j + shift) % dp_count) for j in range(dp_count)]))
    rows_all = jnp.stack(arrived, axis=0)
    gate_mat, up_mat, down_mat = w_gate[0], w_up[0], w_down[0]
    gate_pre = jnp.dot(rows_in, gate_mat, preferred_element_type=jnp.float32)
    up_pre = jnp.dot(rows_in, up_mat, preferred_element_type=jnp.float32)
    sigma = jax.nn.sigmoid(gate_pre)
    silu_value = gate_pre * sigma
    hidden = (silu_value * up_pre).astype(jnp.bfloat16)
    expert_out = jnp.dot(hidden, down_mat, preferred_element_type=jnp.float32).astype(jnp.bfloat16)
    grads_in, rows_all = lax.optimization_barrier((grads_in, rows_all))
    grad_hidden = contract_last(grads_in, down_mat)
    slope = sigma * (1.0 + gate_pre * (1.0 - sigma))
    grad_gate_pre = (grad_hidden * up_pre * slope).astype(jnp.bfloat16)
    grad_up_pre = (grad_hidden * silu_value).astype(jnp.bfloat16)
    pair_grad = (
        contract_last(grad_gate_pre, gate_mat) + contract_last(grad_up_pre, up_mat)
    ).astype(jnp.bfloat16)
    back_out, back_grad = (
        lax.all_to_all(
            expert_out.reshape(flat_shape),
            ("outer", "inner"),
            split_axis=0,
            concat_axis=0,
            tiled=True,
        ),
        lax.all_to_all(
            pair_grad.reshape(flat_shape),
            ("outer", "inner"),
            split_axis=0,
            concat_axis=0,
            tiled=True,
        ),
    )
    joined_grads = jnp.concatenate([grad_gate_pre, grad_up_pre], axis=1)
    source_order = (dp_index - jnp.arange(dp_count)) % dp_count
    joined_all = jnp.take(lax.all_gather(joined_grads, "dp", axis=0, tiled=False), source_order, axis=0)
    grad_joined = lax.dot_general(
        rows_all, joined_all, (((0, 1), (0, 1)), ((), ())), preferred_element_type=jnp.float32
    )
    columns = grads_in
    grad_down = (
        lax.psum_scatter(
            contract_first(columns, hidden).astype(jnp.bfloat16),
            "dp",
            scatter_dimension=0,
            tiled=True,
        )
        .astype(jnp.float32)
        .T
    )
    pair_out = back_out.reshape(-1, width)[pair_slot].reshape(local_tokens, top_count, width)
    pair_back = back_grad.reshape(-1, width)[pair_slot].reshape(local_tokens, top_count, width)
    output = jnp.sum(gate_values[:, :, None] * pair_out.astype(jnp.float32), axis=1).astype(
        jnp.bfloat16
    )
    grad_tokens = jnp.sum(pair_back.astype(jnp.float32), axis=1).astype(jnp.bfloat16)
    grad_gates = jnp.einsum("tkd,td->tk", pair_out, upstream, preferred_element_type=jnp.float32)
    grad_w_gate = grad_joined[:, :ff_width].astype(jnp.bfloat16)[None]
    grad_w_up = grad_joined[:, ff_width:].astype(jnp.bfloat16)[None]
    grad_w_down = grad_down.astype(jnp.bfloat16)[None]
    return (output, grad_tokens, grad_gates, grad_w_gate, grad_w_up, grad_w_down)


def solution(mesh):
    placed = (
        P(("dp", "outer", "inner"), None),
        P(("dp", "outer", "inner"), None),
        P(("dp", "outer", "inner"), None),
        P(("dp", "outer", "inner"), None),
        P(("outer", "inner"), None, None),
        P(("outer", "inner"), None, None),
        P(("outer", "inner"), None, None),
    )
    return jax.shard_map(
        local,
        mesh=mesh,
        in_specs=placed,
        out_specs=(
            P(("dp", "outer", "inner"), None),
            P(("dp", "outer", "inner"), None),
            P(("dp", "outer", "inner"), None),
            P(("outer", "inner"), "dp", None),
            P(("outer", "inner"), "dp", None),
            P(("outer", "inner"), None, "dp"),
        ),
        check_vma=False,
    )
```

```python
import jax
import jax.numpy as jnp
from jax import lax
from jax.sharding import PartitionSpec as P


def contract_last(left, right):
    return lax.dot_general(
        left, right, (((1,), (1,)), ((), ())), preferred_element_type=jnp.float32
    )


def contract_first(left, right):
    return lax.dot_general(
        left, right, (((0,), (0,)), ((), ())), preferred_element_type=jnp.float32
    )


def expert_rows(rows_in, grads_in, gate_mat, up_mat, down_mat):
    gate_pre = jnp.dot(rows_in, gate_mat, preferred_element_type=jnp.float32)
    up_pre = jnp.dot(rows_in, up_mat, preferred_element_type=jnp.float32)
    sigma = jax.nn.sigmoid(gate_pre)
    silu_value = gate_pre * sigma
    hidden = (silu_value * up_pre).astype(jnp.bfloat16)
    expert_out = jnp.dot(hidden, down_mat, preferred_element_type=jnp.float32).astype(jnp.bfloat16)
    grad_hidden = contract_last(grads_in, down_mat)
    slope = sigma * (1.0 + gate_pre * (1.0 - sigma))
    grad_gate_pre = (grad_hidden * up_pre * slope).astype(jnp.bfloat16)
    grad_up_pre = (grad_hidden * silu_value).astype(jnp.bfloat16)
    pair_grad = (
        contract_last(grad_gate_pre, gate_mat) + contract_last(grad_up_pre, up_mat)
    ).astype(jnp.bfloat16)
    return (hidden, expert_out, grad_gate_pre, grad_up_pre, pair_grad)


def local(tokens, expert_ids, gate_values, upstream, w_gate, w_up, w_down):
    local_tokens = tokens.shape[0]
    width = tokens.shape[1]
    top_count = expert_ids.shape[1]
    ff_width = w_gate.shape[2]
    outer_count = lax.axis_size("outer")
    inner_count = lax.axis_size("inner")
    expert_count = outer_count * inner_count
    capacity = min(local_tokens, 3 * local_tokens * top_count // (2 * expert_count))
    pair_count = local_tokens * top_count
    flat_ids = expert_ids.reshape(-1)
    flat_gates = gate_values.reshape(-1)
    onehot = (flat_ids[:, None] == jnp.arange(expert_count, dtype=jnp.int32)[None, :]).astype(
        jnp.int32
    )
    slot_rank = jnp.sum((jnp.cumsum(onehot, axis=0) - onehot) * onehot, axis=1)
    pair_slot = flat_ids * capacity + slot_rank
    slot_pair = (
        jnp.full((expert_count * capacity,), pair_count, jnp.int32)
        .at[pair_slot]
        .set(jnp.arange(pair_count, dtype=jnp.int32))
    )
    slot_token = jnp.where(slot_pair < pair_count, slot_pair // top_count, local_tokens)
    token_pad = jnp.concatenate([tokens, jnp.zeros((1, width), jnp.bfloat16)], axis=0)
    upstream_pad = jnp.concatenate([upstream, jnp.zeros((1, width), jnp.bfloat16)], axis=0)
    gate_pad = jnp.concatenate([flat_gates, jnp.zeros((1,), jnp.float32)], axis=0)
    send_rows = token_pad[slot_token]
    send_grads = (
        gate_pad[slot_pair][:, None] * upstream_pad[slot_token].astype(jnp.float32)
    ).astype(jnp.bfloat16)
    fold = 1
    while (capacity * fold) % 16 or (width // fold) % 128 or width % fold:
        fold += 1
    if (width // fold) % 128 or width % fold:
        fold = 1
    flat_shape = (expert_count, capacity * fold, width // fold)
    got_rows, got_grads = (
        lax.all_to_all(
            send_rows.reshape(flat_shape),
            ("outer", "inner"),
            split_axis=0,
            concat_axis=0,
            tiled=True,
        ),
        lax.all_to_all(
            send_grads.reshape(flat_shape),
            ("outer", "inner"),
            split_axis=0,
            concat_axis=0,
            tiled=True,
        ),
    )
    rows_in = got_rows.reshape(-1, width)
    grads_in = got_grads.reshape(-1, width)
    dp_count = lax.axis_size("dp")
    piece = width // dp_count
    dp_index = lax.axis_index("dp")
    arrived = [lax.dynamic_slice_in_dim(rows_in, dp_index * piece, piece, axis=1)]
    for shift in range(1, dp_count):
        outgoing = lax.dynamic_slice_in_dim(rows_in, ((dp_index + shift) % dp_count) * piece, piece, axis=1)
        arrived.append(lax.ppermute(outgoing, "dp", [(j, (j + shift) % dp_count) for j in range(dp_count)]))
    rows_all = jnp.stack(arrived, axis=0)
    gate_mat, up_mat, down_mat = w_gate[0], w_up[0], w_down[0]
    gate_pre = jnp.dot(rows_in, gate_mat, preferred_element_type=jnp.float32)
    up_pre = jnp.dot(rows_in, up_mat, preferred_element_type=jnp.float32)
    sigma = jax.nn.sigmoid(gate_pre)
    silu_value = gate_pre * sigma
    hidden = (silu_value * up_pre).astype(jnp.bfloat16)
    expert_out = jnp.dot(hidden, down_mat, preferred_element_type=jnp.float32).astype(jnp.bfloat16)
    grads_in, rows_all, expert_out = lax.optimization_barrier((grads_in, rows_all, expert_out))
    grad_hidden = contract_last(grads_in, down_mat)
    slope = sigma * (1.0 + gate_pre * (1.0 - sigma))
    grad_gate_pre = (grad_hidden * up_pre * slope).astype(jnp.bfloat16)
    grad_up_pre = (grad_hidden * silu_value).astype(jnp.bfloat16)
    pair_grad = (
        contract_last(grad_gate_pre, gate_mat) + contract_last(grad_up_pre, up_mat)
    ).astype(jnp.bfloat16)
    back_out, back_grad = (
        lax.all_to_all(
            expert_out.reshape(flat_shape),
            ("outer", "inner"),
            split_axis=0,
            concat_axis=0,
            tiled=True,
        ),
        lax.all_to_all(
            pair_grad.reshape(flat_shape),
            ("outer", "inner"),
            split_axis=0,
            concat_axis=0,
            tiled=True,
        ),
    )
    joined_grads = jnp.concatenate([grad_gate_pre, grad_up_pre], axis=1)
    source_order = (dp_index - jnp.arange(dp_count)) % dp_count
    joined_all = jnp.take(lax.all_gather(joined_grads, "dp", axis=0, tiled=False), source_order, axis=0)
    grad_joined = lax.dot_general(
        rows_all, joined_all, (((0, 1), (0, 1)), ((), ())), preferred_element_type=jnp.float32
    )
    columns = grads_in
    grad_down = (
        lax.psum_scatter(
            contract_first(columns, hidden).astype(jnp.bfloat16),
            "dp",
            scatter_dimension=0,
            tiled=True,
        )
        .astype(jnp.float32)
        .T
    )
    pair_out = back_out.reshape(-1, width)[pair_slot].reshape(local_tokens, top_count, width)
    pair_back = back_grad.reshape(-1, width)[pair_slot].reshape(local_tokens, top_count, width)
    output = jnp.sum(gate_values[:, :, None] * pair_out.astype(jnp.float32), axis=1).astype(
        jnp.bfloat16
    )
    grad_tokens = jnp.sum(pair_back.astype(jnp.float32), axis=1).astype(jnp.bfloat16)
    grad_gates = jnp.einsum("tkd,td->tk", pair_out, upstream, preferred_element_type=jnp.float32)
    grad_w_gate = grad_joined[:, :ff_width].astype(jnp.bfloat16)[None]
    grad_w_up = grad_joined[:, ff_width:].astype(jnp.bfloat16)[None]
    grad_w_down = grad_down.astype(jnp.bfloat16)[None]
    return (output, grad_tokens, grad_gates, grad_w_gate, grad_w_up, grad_w_down)


def solution(mesh):
    placed = (
        P(("dp", "outer", "inner"), None),
        P(("dp", "outer", "inner"), None),
        P(("dp", "outer", "inner"), None),
        P(("dp", "outer", "inner"), None),
        P(("outer", "inner"), None, None),
        P(("outer", "inner"), None, None),
        P(("outer", "inner"), None, None),
    )
    return jax.shard_map(
        local,
        mesh=mesh,
        in_specs=placed,
        out_specs=(
            P(("dp", "outer", "inner"), None),
            P(("dp", "outer", "inner"), None),
            P(("dp", "outer", "inner"), None),
            P(("outer", "inner"), "dp", None),
            P(("outer", "inner"), "dp", None),
            P(("outer", "inner"), None, "dp"),
        ),
        check_vma=False,
    )
```

```python
import jax
import jax.numpy as jnp
from jax import lax
from jax.sharding import PartitionSpec as P


def contract_last(left, right):
    return lax.dot_general(
        left, right, (((1,), (1,)), ((), ())), preferred_element_type=jnp.float32
    )


def contract_first(left, right):
    return lax.dot_general(
        left, right, (((0,), (0,)), ((), ())), preferred_element_type=jnp.float32
    )


def expert_rows(rows_in, grads_in, gate_mat, up_mat, down_mat):
    gate_pre = jnp.dot(rows_in, gate_mat, preferred_element_type=jnp.float32)
    up_pre = jnp.dot(rows_in, up_mat, preferred_element_type=jnp.float32)
    sigma = jax.nn.sigmoid(gate_pre)
    silu_value = gate_pre * sigma
    hidden = (silu_value * up_pre).astype(jnp.bfloat16)
    expert_out = jnp.dot(hidden, down_mat, preferred_element_type=jnp.float32).astype(jnp.bfloat16)
    grad_hidden = contract_last(grads_in, down_mat)
    slope = sigma * (1.0 + gate_pre * (1.0 - sigma))
    grad_gate_pre = (grad_hidden * up_pre * slope).astype(jnp.bfloat16)
    grad_up_pre = (grad_hidden * silu_value).astype(jnp.bfloat16)
    pair_grad = (
        contract_last(grad_gate_pre, gate_mat) + contract_last(grad_up_pre, up_mat)
    ).astype(jnp.bfloat16)
    return (hidden, expert_out, grad_gate_pre, grad_up_pre, pair_grad)


def local(tokens, expert_ids, gate_values, upstream, w_gate, w_up, w_down):
    local_tokens = tokens.shape[0]
    width = tokens.shape[1]
    top_count = expert_ids.shape[1]
    ff_width = w_gate.shape[2]
    outer_count = lax.axis_size("outer")
    inner_count = lax.axis_size("inner")
    expert_count = outer_count * inner_count
    capacity = min(local_tokens, 3 * local_tokens * top_count // (2 * expert_count))
    pair_count = local_tokens * top_count
    flat_ids = expert_ids.reshape(-1)
    flat_gates = gate_values.reshape(-1)
    onehot = (flat_ids[:, None] == jnp.arange(expert_count, dtype=jnp.int32)[None, :]).astype(
        jnp.int32
    )
    slot_rank = jnp.sum((jnp.cumsum(onehot, axis=0) - onehot) * onehot, axis=1)
    pair_slot = flat_ids * capacity + slot_rank
    slot_pair = (
        jnp.full((expert_count * capacity,), pair_count, jnp.int32)
        .at[pair_slot]
        .set(jnp.arange(pair_count, dtype=jnp.int32))
    )
    slot_token = jnp.where(slot_pair < pair_count, slot_pair // top_count, local_tokens)
    token_pad = jnp.concatenate([tokens, jnp.zeros((1, width), jnp.bfloat16)], axis=0)
    upstream_pad = jnp.concatenate([upstream, jnp.zeros((1, width), jnp.bfloat16)], axis=0)
    gate_pad = jnp.concatenate([flat_gates, jnp.zeros((1,), jnp.float32)], axis=0)
    fold = 1
    while (capacity * fold) % 16 or (width // fold) % 128 or width % fold:
        fold += 1
    if (width // fold) % 128 or width % fold:
        fold = 1
    narrow = width // fold
    flat_shape = (expert_count, capacity * fold, narrow)
    row_index = (slot_token[:, None] * fold + jnp.arange(fold, dtype=jnp.int32)[None, :]).reshape(-1)
    send_rows = token_pad.reshape(-1, narrow)[row_index]
    send_grads = (
        jnp.repeat(gate_pad[slot_pair], fold)[:, None]
        * upstream_pad.reshape(-1, narrow)[row_index].astype(jnp.float32)
    ).astype(jnp.bfloat16)
    got_rows, got_grads = (
        lax.all_to_all(
            send_rows.reshape(flat_shape),
            ("outer", "inner"),
            split_axis=0,
            concat_axis=0,
            tiled=True,
        ),
        lax.all_to_all(
            send_grads.reshape(flat_shape),
            ("outer", "inner"),
            split_axis=0,
            concat_axis=0,
            tiled=True,
        ),
    )
    rows_in = got_rows.reshape(-1, width)
    grads_in = got_grads.reshape(-1, width)
    dp_count = lax.axis_size("dp")
    piece = width // dp_count
    dp_index = lax.axis_index("dp")
    arrived = [lax.dynamic_slice_in_dim(rows_in, dp_index * piece, piece, axis=1)]
    for shift in range(1, dp_count):
        outgoing = lax.dynamic_slice_in_dim(rows_in, ((dp_index + shift) % dp_count) * piece, piece, axis=1)
        arrived.append(lax.ppermute(outgoing, "dp", [(j, (j + shift) % dp_count) for j in range(dp_count)]))
    rows_all = jnp.stack(arrived, axis=0)
    gate_mat, up_mat, down_mat = w_gate[0], w_up[0], w_down[0]
    gate_pre = jnp.dot(rows_in, gate_mat, preferred_element_type=jnp.float32)
    up_pre = jnp.dot(rows_in, up_mat, preferred_element_type=jnp.float32)
    sigma = jax.nn.sigmoid(gate_pre)
    silu_value = gate_pre * sigma
    hidden = (silu_value * up_pre).astype(jnp.bfloat16)
    expert_out = jnp.dot(hidden, down_mat, preferred_element_type=jnp.float32).astype(jnp.bfloat16)
    grads_in, rows_all, expert_out = lax.optimization_barrier((grads_in, rows_all, expert_out))
    grad_hidden = contract_last(grads_in, down_mat)
    slope = sigma * (1.0 + gate_pre * (1.0 - sigma))
    grad_gate_pre = (grad_hidden * up_pre * slope).astype(jnp.bfloat16)
    grad_up_pre = (grad_hidden * silu_value).astype(jnp.bfloat16)
    pair_grad = (
        contract_last(grad_gate_pre, gate_mat) + contract_last(grad_up_pre, up_mat)
    ).astype(jnp.bfloat16)
    back_out, back_grad = (
        lax.all_to_all(
            expert_out.reshape(flat_shape),
            ("outer", "inner"),
            split_axis=0,
            concat_axis=0,
            tiled=True,
        ),
        lax.all_to_all(
            pair_grad.reshape(flat_shape),
            ("outer", "inner"),
            split_axis=0,
            concat_axis=0,
            tiled=True,
        ),
    )
    joined_grads = jnp.concatenate([grad_gate_pre, grad_up_pre], axis=1)
    source_order = (dp_index - jnp.arange(dp_count)) % dp_count
    joined_all = jnp.take(lax.all_gather(joined_grads, "dp", axis=0, tiled=False), source_order, axis=0)
    grad_joined = lax.dot_general(
        rows_all, joined_all, (((0, 1), (0, 1)), ((), ())), preferred_element_type=jnp.float32
    )
    columns = grads_in
    grad_down = (
        lax.psum_scatter(
            contract_first(columns, hidden).astype(jnp.bfloat16),
            "dp",
            scatter_dimension=0,
            tiled=True,
        )
        .astype(jnp.float32)
        .T
    )
    pair_index = (
        pair_slot.reshape(local_tokens, 1, top_count) * fold
        + jnp.arange(fold, dtype=jnp.int32)[None, :, None]
    ).reshape(local_tokens * fold, top_count)
    pair_out = back_out.reshape(-1, narrow)[pair_index].astype(jnp.float32)
    pair_back = back_grad.reshape(-1, narrow)[pair_index].astype(jnp.float32)
    gate_rows = jnp.repeat(gate_values, fold, axis=0)
    output = (
        jnp.sum(gate_rows[:, :, None] * pair_out, axis=1).reshape(local_tokens, width).astype(jnp.bfloat16)
    )
    grad_tokens = jnp.sum(pair_back, axis=1).reshape(local_tokens, width).astype(jnp.bfloat16)
    upstream_rows = upstream.reshape(local_tokens * fold, narrow).astype(jnp.float32)
    grad_gates = jnp.sum(
        jnp.sum(upstream_rows[:, None, :] * pair_out, axis=2).reshape(local_tokens, fold, top_count),
        axis=1,
    )
    grad_w_gate = grad_joined[:, :ff_width].astype(jnp.bfloat16)[None]
    grad_w_up = grad_joined[:, ff_width:].astype(jnp.bfloat16)[None]
    grad_w_down = grad_down.astype(jnp.bfloat16)[None]
    return (output, grad_tokens, grad_gates, grad_w_gate, grad_w_up, grad_w_down)


def solution(mesh):
    placed = (
        P(("dp", "outer", "inner"), None),
        P(("dp", "outer", "inner"), None),
        P(("dp", "outer", "inner"), None),
        P(("dp", "outer", "inner"), None),
        P(("outer", "inner"), None, None),
        P(("outer", "inner"), None, None),
        P(("outer", "inner"), None, None),
    )
    return jax.shard_map(
        local,
        mesh=mesh,
        in_specs=placed,
        out_specs=(
            P(("dp", "outer", "inner"), None),
            P(("dp", "outer", "inner"), None),
            P(("dp", "outer", "inner"), None),
            P(("outer", "inner"), "dp", None),
            P(("outer", "inner"), "dp", None),
            P(("outer", "inner"), None, "dp"),
        ),
        check_vma=False,
    )
```

```python
import jax
import jax.numpy as jnp
from jax import lax
from jax.sharding import PartitionSpec as P


def contract_last(left, right):
    return lax.dot_general(
        left, right, (((1,), (1,)), ((), ())), preferred_element_type=jnp.float32
    )


def contract_first(left, right):
    return lax.dot_general(
        left, right, (((0,), (0,)), ((), ())), preferred_element_type=jnp.float32
    )


def expert_rows(rows_in, grads_in, gate_mat, up_mat, down_mat):
    gate_pre = jnp.dot(rows_in, gate_mat, preferred_element_type=jnp.float32)
    up_pre = jnp.dot(rows_in, up_mat, preferred_element_type=jnp.float32)
    sigma = jax.nn.sigmoid(gate_pre)
    silu_value = gate_pre * sigma
    hidden = (silu_value * up_pre).astype(jnp.bfloat16)
    expert_out = jnp.dot(hidden, down_mat, preferred_element_type=jnp.float32).astype(jnp.bfloat16)
    grad_hidden = contract_last(grads_in, down_mat)
    slope = sigma * (1.0 + gate_pre * (1.0 - sigma))
    grad_gate_pre = (grad_hidden * up_pre * slope).astype(jnp.bfloat16)
    grad_up_pre = (grad_hidden * silu_value).astype(jnp.bfloat16)
    pair_grad = (
        contract_last(grad_gate_pre, gate_mat) + contract_last(grad_up_pre, up_mat)
    ).astype(jnp.bfloat16)
    return (hidden, expert_out, grad_gate_pre, grad_up_pre, pair_grad)


def local(tokens, expert_ids, gate_values, upstream, w_gate, w_up, w_down):
    local_tokens = tokens.shape[0]
    width = tokens.shape[1]
    top_count = expert_ids.shape[1]
    ff_width = w_gate.shape[2]
    outer_count = lax.axis_size("outer")
    inner_count = lax.axis_size("inner")
    expert_count = outer_count * inner_count
    capacity = min(local_tokens, 3 * local_tokens * top_count // (2 * expert_count))
    pair_count = local_tokens * top_count
    flat_ids = expert_ids.reshape(-1)
    flat_gates = gate_values.reshape(-1)
    onehot = (flat_ids[:, None] == jnp.arange(expert_count, dtype=jnp.int32)[None, :]).astype(
        jnp.int32
    )
    slot_rank = jnp.sum((jnp.cumsum(onehot, axis=0) - onehot) * onehot, axis=1)
    pair_slot = flat_ids * capacity + slot_rank
    slot_pair = (
        jnp.full((expert_count * capacity,), pair_count, jnp.int32)
        .at[pair_slot]
        .set(jnp.arange(pair_count, dtype=jnp.int32))
    )
    slot_token = jnp.where(slot_pair < pair_count, slot_pair // top_count, local_tokens)
    token_pad = jnp.concatenate([tokens, jnp.zeros((1, width), jnp.bfloat16)], axis=0)
    upstream_pad = jnp.concatenate([upstream, jnp.zeros((1, width), jnp.bfloat16)], axis=0)
    gate_pad = jnp.concatenate([flat_gates, jnp.zeros((1,), jnp.float32)], axis=0)
    fold = 1
    while (capacity * fold) % 16 or (width // fold) % 128 or width % fold:
        fold += 1
    if (width // fold) % 128 or width % fold:
        fold = 1
    narrow = width // fold
    flat_shape = (expert_count, capacity * fold, narrow)
    row_index = (slot_token[:, None] * fold + jnp.arange(fold, dtype=jnp.int32)[None, :]).reshape(-1)
    send_rows = token_pad.reshape(-1, narrow)[row_index]
    send_grads = (
        jnp.repeat(gate_pad[slot_pair], fold)[:, None]
        * upstream_pad.reshape(-1, narrow)[row_index].astype(jnp.float32)
    ).astype(jnp.bfloat16)
    got_rows, got_grads = (
        lax.all_to_all(
            send_rows.reshape(flat_shape),
            ("outer", "inner"),
            split_axis=0,
            concat_axis=0,
            tiled=True,
        ),
        lax.all_to_all(
            send_grads.reshape(flat_shape),
            ("outer", "inner"),
            split_axis=0,
            concat_axis=0,
            tiled=True,
        ),
    )
    rows_in = got_rows.reshape(-1, width)
    grads_in = got_grads.reshape(-1, width)
    dp_count = lax.axis_size("dp")
    piece = width // dp_count
    dp_index = lax.axis_index("dp")
    arrived = [lax.dynamic_slice_in_dim(rows_in, dp_index * piece, piece, axis=1)]
    for shift in range(1, dp_count):
        outgoing = lax.dynamic_slice_in_dim(rows_in, ((dp_index + shift) % dp_count) * piece, piece, axis=1)
        arrived.append(lax.ppermute(outgoing, "dp", [(j, (j + shift) % dp_count) for j in range(dp_count)]))
    rows_all = jnp.stack(arrived, axis=0)
    gate_mat, up_mat, down_mat = w_gate[0], w_up[0], w_down[0]
    gate_pre = jnp.dot(rows_in, gate_mat, preferred_element_type=jnp.float32)
    up_pre = jnp.dot(rows_in, up_mat, preferred_element_type=jnp.float32)
    sigma = jax.nn.sigmoid(gate_pre)
    silu_value = gate_pre * sigma
    hidden = (silu_value * up_pre).astype(jnp.bfloat16)
    expert_out = jnp.dot(hidden, down_mat, preferred_element_type=jnp.float32).astype(jnp.bfloat16)
    grads_in, rows_all, expert_out = lax.optimization_barrier((grads_in, rows_all, expert_out))
    grad_hidden = contract_last(grads_in, down_mat)
    slope = sigma * (1.0 + gate_pre * (1.0 - sigma))
    grad_gate_pre = (grad_hidden * up_pre * slope).astype(jnp.bfloat16)
    grad_up_pre = (grad_hidden * silu_value).astype(jnp.bfloat16)
    pair_grad = (
        contract_last(grad_gate_pre, gate_mat) + contract_last(grad_up_pre, up_mat)
    ).astype(jnp.bfloat16)
    back_out, back_grad = (
        lax.all_to_all(
            expert_out.reshape(flat_shape),
            ("outer", "inner"),
            split_axis=0,
            concat_axis=0,
            tiled=True,
        ),
        lax.all_to_all(
            pair_grad.reshape(flat_shape),
            ("outer", "inner"),
            split_axis=0,
            concat_axis=0,
            tiled=True,
        ),
    )
    joined_grads = jnp.concatenate([grad_gate_pre, grad_up_pre], axis=1)
    joined_arrived = [joined_grads]
    for shift in range(1, dp_count):
        joined_arrived.append(
            lax.ppermute(joined_grads, "dp", [(j, (j + shift) % dp_count) for j in range(dp_count)])
        )
    joined_all = jnp.stack(joined_arrived, axis=0)
    grad_joined = lax.dot_general(
        rows_all, joined_all, (((0, 1), (0, 1)), ((), ())), preferred_element_type=jnp.float32
    )
    columns = grads_in
    grad_down = (
        lax.psum_scatter(
            contract_first(columns, hidden).astype(jnp.bfloat16),
            "dp",
            scatter_dimension=0,
            tiled=True,
        )
        .astype(jnp.float32)
        .T
    )
    pair_index = (
        pair_slot.reshape(local_tokens, 1, top_count) * fold
        + jnp.arange(fold, dtype=jnp.int32)[None, :, None]
    ).reshape(local_tokens * fold, top_count)
    pair_out = back_out.reshape(-1, narrow)[pair_index].astype(jnp.float32)
    grad_joined, back_grad = lax.optimization_barrier((grad_joined, back_grad))
    pair_back = back_grad.reshape(-1, narrow)[pair_index].astype(jnp.float32)
    gate_rows = jnp.repeat(gate_values, fold, axis=0)
    output = (
        jnp.sum(gate_rows[:, :, None] * pair_out, axis=1).reshape(local_tokens, width).astype(jnp.bfloat16)
    )
    grad_tokens = jnp.sum(pair_back, axis=1).reshape(local_tokens, width).astype(jnp.bfloat16)
    upstream_rows = upstream.reshape(local_tokens * fold, narrow).astype(jnp.float32)
    grad_gates = jnp.sum(
        jnp.sum(upstream_rows[:, None, :] * pair_out, axis=2).reshape(local_tokens, fold, top_count),
        axis=1,
    )
    grad_w_gate = grad_joined[:, :ff_width].astype(jnp.bfloat16)[None]
    grad_w_up = grad_joined[:, ff_width:].astype(jnp.bfloat16)[None]
    grad_w_down = grad_down.astype(jnp.bfloat16)[None]
    return (output, grad_tokens, grad_gates, grad_w_gate, grad_w_up, grad_w_down)


def solution(mesh):
    placed = (
        P(("dp", "outer", "inner"), None),
        P(("dp", "outer", "inner"), None),
        P(("dp", "outer", "inner"), None),
        P(("dp", "outer", "inner"), None),
        P(("outer", "inner"), None, None),
        P(("outer", "inner"), None, None),
        P(("outer", "inner"), None, None),
    )
    return jax.shard_map(
        local,
        mesh=mesh,
        in_specs=placed,
        out_specs=(
            P(("dp", "outer", "inner"), None),
            P(("dp", "outer", "inner"), None),
            P(("dp", "outer", "inner"), None),
            P(("outer", "inner"), "dp", None),
            P(("outer", "inner"), "dp", None),
            P(("outer", "inner"), None, "dp"),
        ),
        check_vma=False,
    )
```

```python
import jax
import jax.numpy as jnp
from jax import lax
from jax.sharding import PartitionSpec as P


def contract_last(left, right):
    return lax.dot_general(
        left, right, (((1,), (1,)), ((), ())), preferred_element_type=jnp.float32
    )


def contract_first(left, right):
    return lax.dot_general(
        left, right, (((0,), (0,)), ((), ())), preferred_element_type=jnp.float32
    )


def expert_rows(rows_in, grads_in, gate_mat, up_mat, down_mat):
    gate_pre = jnp.dot(rows_in, gate_mat, preferred_element_type=jnp.float32)
    up_pre = jnp.dot(rows_in, up_mat, preferred_element_type=jnp.float32)
    sigma = jax.nn.sigmoid(gate_pre)
    silu_value = gate_pre * sigma
    hidden = (silu_value * up_pre).astype(jnp.bfloat16)
    expert_out = jnp.dot(hidden, down_mat, preferred_element_type=jnp.float32).astype(jnp.bfloat16)
    grad_hidden = contract_last(grads_in, down_mat)
    slope = sigma * (1.0 + gate_pre * (1.0 - sigma))
    grad_gate_pre = (grad_hidden * up_pre * slope).astype(jnp.bfloat16)
    grad_up_pre = (grad_hidden * silu_value).astype(jnp.bfloat16)
    pair_grad = (
        contract_last(grad_gate_pre, gate_mat) + contract_last(grad_up_pre, up_mat)
    ).astype(jnp.bfloat16)
    return (hidden, expert_out, grad_gate_pre, grad_up_pre, pair_grad)


def local(tokens, expert_ids, gate_values, upstream, w_gate, w_up, w_down):
    local_tokens = tokens.shape[0]
    width = tokens.shape[1]
    top_count = expert_ids.shape[1]
    ff_width = w_gate.shape[2]
    outer_count = lax.axis_size("outer")
    inner_count = lax.axis_size("inner")
    expert_count = outer_count * inner_count
    capacity = min(local_tokens, 3 * local_tokens * top_count // (2 * expert_count))
    pair_count = local_tokens * top_count
    flat_ids = expert_ids.reshape(-1)
    flat_gates = gate_values.reshape(-1)
    onehot = (flat_ids[:, None] == jnp.arange(expert_count, dtype=jnp.int32)[None, :]).astype(
        jnp.int32
    )
    slot_rank = jnp.sum((jnp.cumsum(onehot, axis=0) - onehot) * onehot, axis=1)
    pair_slot = flat_ids * capacity + slot_rank
    slot_pair = (
        jnp.full((expert_count * capacity,), pair_count, jnp.int32)
        .at[pair_slot]
        .set(jnp.arange(pair_count, dtype=jnp.int32))
    )
    slot_token = jnp.where(slot_pair < pair_count, slot_pair // top_count, local_tokens)
    token_pad = jnp.concatenate([tokens, jnp.zeros((1, width), jnp.bfloat16)], axis=0)
    upstream_pad = jnp.concatenate([upstream, jnp.zeros((1, width), jnp.bfloat16)], axis=0)
    gate_pad = jnp.concatenate([flat_gates, jnp.zeros((1,), jnp.float32)], axis=0)
    fold = 1
    while (capacity * fold) % 16 or (width // fold) % 128 or width % fold:
        fold += 1
    if (width // fold) % 128 or width % fold:
        fold = 1
    narrow = width // fold
    flat_shape = (expert_count, capacity * fold, narrow)
    row_index = (slot_token[:, None] * fold + jnp.arange(fold, dtype=jnp.int32)[None, :]).reshape(-1)
    send_rows = token_pad.reshape(-1, narrow)[row_index]
    send_grads = (
        jnp.repeat(gate_pad[slot_pair], fold)[:, None]
        * upstream_pad.reshape(-1, narrow)[row_index].astype(jnp.float32)
    ).astype(jnp.bfloat16)
    got_rows, got_grads = (
        lax.all_to_all(
            send_rows.reshape(flat_shape),
            ("outer", "inner"),
            split_axis=0,
            concat_axis=0,
            tiled=True,
        ),
        lax.all_to_all(
            send_grads.reshape(flat_shape),
            ("outer", "inner"),
            split_axis=0,
            concat_axis=0,
            tiled=True,
        ),
    )
    rows_in = got_rows.reshape(-1, width)
    grads_in = got_grads.reshape(-1, width)
    dp_count = lax.axis_size("dp")
    piece = width // dp_count
    dp_index = lax.axis_index("dp")
    arrived = [lax.dynamic_slice_in_dim(rows_in, dp_index * piece, piece, axis=1)]
    for shift in range(1, dp_count):
        outgoing = lax.dynamic_slice_in_dim(rows_in, ((dp_index + shift) % dp_count) * piece, piece, axis=1)
        arrived.append(lax.ppermute(outgoing, "dp", [(j, (j + shift) % dp_count) for j in range(dp_count)]))
    rows_all = jnp.stack(arrived, axis=0)
    gate_mat, up_mat, down_mat = w_gate[0], w_up[0], w_down[0]
    gate_pre = jnp.dot(rows_in, gate_mat, preferred_element_type=jnp.float32)
    up_pre = jnp.dot(rows_in, up_mat, preferred_element_type=jnp.float32)
    sigma = jax.nn.sigmoid(gate_pre)
    silu_value = gate_pre * sigma
    hidden = (silu_value * up_pre).astype(jnp.bfloat16)
    expert_out = jnp.dot(hidden, down_mat, preferred_element_type=jnp.float32).astype(jnp.bfloat16)
    grads_in, rows_all, expert_out = lax.optimization_barrier((grads_in, rows_all, expert_out))
    grad_hidden = contract_last(grads_in, down_mat)
    slope = sigma * (1.0 + gate_pre * (1.0 - sigma))
    grad_gate_pre = (grad_hidden * up_pre * slope).astype(jnp.bfloat16)
    grad_up_pre = (grad_hidden * silu_value).astype(jnp.bfloat16)
    pair_grad = (
        contract_last(grad_gate_pre, gate_mat) + contract_last(grad_up_pre, up_mat)
    ).astype(jnp.bfloat16)
    back_out, back_grad = (
        lax.all_to_all(
            expert_out.reshape(flat_shape),
            ("outer", "inner"),
            split_axis=0,
            concat_axis=0,
            tiled=True,
        ),
        lax.all_to_all(
            pair_grad.reshape(flat_shape),
            ("outer", "inner"),
            split_axis=0,
            concat_axis=0,
            tiled=True,
        ),
    )
    joined_grads = jnp.concatenate([grad_gate_pre, grad_up_pre], axis=1)
    source_order = (dp_index - jnp.arange(dp_count)) % dp_count
    joined_all = jnp.take(lax.all_gather(joined_grads, "dp", axis=0, tiled=False), source_order, axis=0)
    grad_joined = lax.dot_general(
        rows_all, joined_all, (((0, 1), (0, 1)), ((), ())), preferred_element_type=jnp.float32
    )
    columns = grads_in
    grad_down = (
        lax.psum_scatter(
            contract_first(columns, hidden).astype(jnp.bfloat16),
            "dp",
            scatter_dimension=0,
            tiled=True,
        )
        .astype(jnp.float32)
        .T
    )
    pair_index = (
        pair_slot.reshape(local_tokens, 1, top_count) * fold
        + jnp.arange(fold, dtype=jnp.int32)[None, :, None]
    ).reshape(local_tokens * fold, top_count)
    pair_out = back_out.reshape(-1, narrow)[pair_index].astype(jnp.float32)
    grad_joined, back_grad = lax.optimization_barrier((grad_joined, back_grad))
    pair_back = back_grad.reshape(-1, narrow)[pair_index].astype(jnp.float32)
    gate_rows = jnp.repeat(gate_values, fold, axis=0)
    output = (
        jnp.sum(gate_rows[:, :, None] * pair_out, axis=1).reshape(local_tokens, width).astype(jnp.bfloat16)
    )
    grad_tokens = jnp.sum(pair_back, axis=1).reshape(local_tokens, width).astype(jnp.bfloat16)
    upstream_rows = upstream.reshape(local_tokens * fold, narrow).astype(jnp.float32)
    grad_gates = jnp.sum(
        jnp.sum(upstream_rows[:, None, :] * pair_out, axis=2).reshape(local_tokens, fold, top_count),
        axis=1,
    )
    grad_w_gate = grad_joined[:, :ff_width].astype(jnp.bfloat16)[None]
    grad_w_up = grad_joined[:, ff_width:].astype(jnp.bfloat16)[None]
    grad_w_down = grad_down.astype(jnp.bfloat16)[None]
    return (output, grad_tokens, grad_gates, grad_w_gate, grad_w_up, grad_w_down)


def solution(mesh):
    placed = (
        P(("dp", "outer", "inner"), None),
        P(("dp", "outer", "inner"), None),
        P(("dp", "outer", "inner"), None),
        P(("dp", "outer", "inner"), None),
        P(("outer", "inner"), None, None),
        P(("outer", "inner"), None, None),
        P(("outer", "inner"), None, None),
    )
    return jax.shard_map(
        local,
        mesh=mesh,
        in_specs=placed,
        out_specs=(
            P(("dp", "outer", "inner"), None),
            P(("dp", "outer", "inner"), None),
            P(("dp", "outer", "inner"), None),
            P(("outer", "inner"), "dp", None),
            P(("outer", "inner"), "dp", None),
            P(("outer", "inner"), None, "dp"),
        ),
        check_vma=False,
    )
```

```python
import jax
import jax.numpy as jnp
from jax import lax
from jax.sharding import PartitionSpec as P


def contract_last(left, right):
    return lax.dot_general(
        left, right, (((1,), (1,)), ((), ())), preferred_element_type=jnp.float32
    )


def contract_first(left, right):
    return lax.dot_general(
        left, right, (((0,), (0,)), ((), ())), preferred_element_type=jnp.float32
    )


def expert_rows(rows_in, grads_in, gate_mat, up_mat, down_mat):
    gate_pre = jnp.dot(rows_in, gate_mat, preferred_element_type=jnp.float32)
    up_pre = jnp.dot(rows_in, up_mat, preferred_element_type=jnp.float32)
    sigma = jax.nn.sigmoid(gate_pre)
    silu_value = gate_pre * sigma
    hidden = (silu_value * up_pre).astype(jnp.bfloat16)
    expert_out = jnp.dot(hidden, down_mat, preferred_element_type=jnp.float32).astype(jnp.bfloat16)
    grad_hidden = contract_last(grads_in, down_mat)
    slope = sigma * (1.0 + gate_pre * (1.0 - sigma))
    grad_gate_pre = (grad_hidden * up_pre * slope).astype(jnp.bfloat16)
    grad_up_pre = (grad_hidden * silu_value).astype(jnp.bfloat16)
    pair_grad = (
        contract_last(grad_gate_pre, gate_mat) + contract_last(grad_up_pre, up_mat)
    ).astype(jnp.bfloat16)
    return (hidden, expert_out, grad_gate_pre, grad_up_pre, pair_grad)


def local(tokens, expert_ids, gate_values, upstream, w_gate, w_up, w_down):
    local_tokens = tokens.shape[0]
    width = tokens.shape[1]
    top_count = expert_ids.shape[1]
    ff_width = w_gate.shape[2]
    outer_count = lax.axis_size("outer")
    inner_count = lax.axis_size("inner")
    expert_count = outer_count * inner_count
    capacity = min(local_tokens, 3 * local_tokens * top_count // (2 * expert_count))
    pair_count = local_tokens * top_count
    flat_ids = expert_ids.reshape(-1)
    flat_gates = gate_values.reshape(-1)
    onehot = (flat_ids[:, None] == jnp.arange(expert_count, dtype=jnp.int32)[None, :]).astype(
        jnp.int32
    )
    slot_rank = jnp.sum((jnp.cumsum(onehot, axis=0) - onehot) * onehot, axis=1)
    pair_slot = flat_ids * capacity + slot_rank
    slot_pair = (
        jnp.full((expert_count * capacity,), pair_count, jnp.int32)
        .at[pair_slot]
        .set(jnp.arange(pair_count, dtype=jnp.int32))
    )
    slot_token = jnp.where(slot_pair < pair_count, slot_pair // top_count, local_tokens)
    token_pad = jnp.concatenate([tokens, jnp.zeros((1, width), jnp.bfloat16)], axis=0)
    upstream_pad = jnp.concatenate([upstream, jnp.zeros((1, width), jnp.bfloat16)], axis=0)
    gate_pad = jnp.concatenate([flat_gates, jnp.zeros((1,), jnp.float32)], axis=0)
    fold = 1
    while (capacity * fold) % 16 or (width // fold) % 128 or width % fold:
        fold += 1
    if (width // fold) % 128 or width % fold:
        fold = 1
    narrow = width // fold
    flat_shape = (expert_count, capacity * fold, narrow)
    row_index = (slot_token[:, None] * fold + jnp.arange(fold, dtype=jnp.int32)[None, :]).reshape(-1)
    send_rows = token_pad.reshape(-1, narrow)[row_index]
    send_grads = (
        jnp.repeat(gate_pad[slot_pair], fold)[:, None]
        * upstream_pad.reshape(-1, narrow)[row_index].astype(jnp.float32)
    ).astype(jnp.bfloat16)
    got_rows, got_grads = (
        lax.all_to_all(
            send_rows.reshape(flat_shape),
            ("outer", "inner"),
            split_axis=0,
            concat_axis=0,
            tiled=True,
        ),
        lax.all_to_all(
            send_grads.reshape(flat_shape),
            ("outer", "inner"),
            split_axis=0,
            concat_axis=0,
            tiled=True,
        ),
    )
    rows_in = got_rows.reshape(-1, width)
    grads_in = got_grads.reshape(-1, width)
    dp_count = lax.axis_size("dp")
    piece = width // dp_count
    dp_index = lax.axis_index("dp")
    arrived = [lax.dynamic_slice_in_dim(rows_in, dp_index * piece, piece, axis=1)]
    for shift in range(1, dp_count):
        outgoing = lax.dynamic_slice_in_dim(rows_in, ((dp_index + shift) % dp_count) * piece, piece, axis=1)
        arrived.append(lax.ppermute(outgoing, "dp", [(j, (j + shift) % dp_count) for j in range(dp_count)]))
    rows_all = jnp.stack(arrived, axis=0)
    gate_mat, up_mat, down_mat = w_gate[0], w_up[0], w_down[0]
    gate_pre = jnp.dot(rows_in, gate_mat, preferred_element_type=jnp.float32)
    up_pre = jnp.dot(rows_in, up_mat, preferred_element_type=jnp.float32)
    sigma = jax.nn.sigmoid(gate_pre)
    silu_value = gate_pre * sigma
    hidden = (silu_value * up_pre).astype(jnp.bfloat16)
    expert_out = jnp.dot(hidden, down_mat, preferred_element_type=jnp.float32).astype(jnp.bfloat16)
    out_send = expert_out.reshape(flat_shape)
    grads_in, rows_all, out_send = lax.optimization_barrier((grads_in, rows_all, out_send))
    grad_hidden = contract_last(grads_in, down_mat)
    slope = sigma * (1.0 + gate_pre * (1.0 - sigma))
    grad_gate_pre = (grad_hidden * up_pre * slope).astype(jnp.bfloat16)
    grad_up_pre = (grad_hidden * silu_value).astype(jnp.bfloat16)
    pair_grad = (
        contract_last(grad_gate_pre, gate_mat) + contract_last(grad_up_pre, up_mat)
    ).astype(jnp.bfloat16)
    back_out, back_grad = (
        lax.all_to_all(
            out_send,
            ("outer", "inner"),
            split_axis=0,
            concat_axis=0,
            tiled=True,
        ),
        lax.all_to_all(
            pair_grad.reshape(flat_shape),
            ("outer", "inner"),
            split_axis=0,
            concat_axis=0,
            tiled=True,
        ),
    )
    joined_grads = jnp.concatenate([grad_gate_pre, grad_up_pre], axis=1)
    source_order = (dp_index - jnp.arange(dp_count)) % dp_count
    joined_all = jnp.take(lax.all_gather(joined_grads, "dp", axis=0, tiled=False), source_order, axis=0)
    grad_joined = lax.dot_general(
        rows_all, joined_all, (((0, 1), (0, 1)), ((), ())), preferred_element_type=jnp.float32
    )
    columns = grads_in
    grad_down = (
        lax.psum_scatter(
            contract_first(columns, hidden).astype(jnp.bfloat16),
            "dp",
            scatter_dimension=0,
            tiled=True,
        )
        .astype(jnp.float32)
        .T
    )
    pair_index = (
        pair_slot.reshape(local_tokens, 1, top_count) * fold
        + jnp.arange(fold, dtype=jnp.int32)[None, :, None]
    ).reshape(local_tokens * fold, top_count)
    pair_out = back_out.reshape(-1, narrow)[pair_index].astype(jnp.float32)
    grad_w_gate = grad_joined[:, :ff_width].astype(jnp.bfloat16)[None]
    grad_w_up = grad_joined[:, ff_width:].astype(jnp.bfloat16)[None]
    grad_w_gate, grad_w_up, back_grad = lax.optimization_barrier((grad_w_gate, grad_w_up, back_grad))
    pair_back = back_grad.reshape(-1, narrow)[pair_index].astype(jnp.float32)
    gate_rows = jnp.repeat(gate_values, fold, axis=0)
    output = (
        jnp.sum(gate_rows[:, :, None] * pair_out, axis=1).reshape(local_tokens, width).astype(jnp.bfloat16)
    )
    grad_tokens = jnp.sum(pair_back, axis=1).reshape(local_tokens, width).astype(jnp.bfloat16)
    upstream_rows = upstream.reshape(local_tokens * fold, narrow).astype(jnp.float32)
    grad_gates = jnp.sum(
        jnp.sum(upstream_rows[:, None, :] * pair_out, axis=2).reshape(local_tokens, fold, top_count),
        axis=1,
    )
    grad_w_down = grad_down.astype(jnp.bfloat16)[None]
    return (output, grad_tokens, grad_gates, grad_w_gate, grad_w_up, grad_w_down)


def solution(mesh):
    placed = (
        P(("dp", "outer", "inner"), None),
        P(("dp", "outer", "inner"), None),
        P(("dp", "outer", "inner"), None),
        P(("dp", "outer", "inner"), None),
        P(("outer", "inner"), None, None),
        P(("outer", "inner"), None, None),
        P(("outer", "inner"), None, None),
    )
    return jax.shard_map(
        local,
        mesh=mesh,
        in_specs=placed,
        out_specs=(
            P(("dp", "outer", "inner"), None),
            P(("dp", "outer", "inner"), None),
            P(("dp", "outer", "inner"), None),
            P(("outer", "inner"), "dp", None),
            P(("outer", "inner"), "dp", None),
            P(("outer", "inner"), None, "dp"),
        ),
        check_vma=False,
    )
```

```python
import jax
import jax.numpy as jnp
from jax import lax
from jax.sharding import PartitionSpec as P


def contract_last(left, right):
    return lax.dot_general(
        left, right, (((1,), (1,)), ((), ())), preferred_element_type=jnp.float32
    )


def contract_first(left, right):
    return lax.dot_general(
        left, right, (((0,), (0,)), ((), ())), preferred_element_type=jnp.float32
    )


def expert_rows(rows_in, grads_in, gate_mat, up_mat, down_mat):
    gate_pre = jnp.dot(rows_in, gate_mat, preferred_element_type=jnp.float32)
    up_pre = jnp.dot(rows_in, up_mat, preferred_element_type=jnp.float32)
    sigma = jax.nn.sigmoid(gate_pre)
    silu_value = gate_pre * sigma
    hidden = (silu_value * up_pre).astype(jnp.bfloat16)
    expert_out = jnp.dot(hidden, down_mat, preferred_element_type=jnp.float32).astype(jnp.bfloat16)
    grad_hidden = contract_last(grads_in, down_mat)
    slope = sigma * (1.0 + gate_pre * (1.0 - sigma))
    grad_gate_pre = (grad_hidden * up_pre * slope).astype(jnp.bfloat16)
    grad_up_pre = (grad_hidden * silu_value).astype(jnp.bfloat16)
    pair_grad = (
        contract_last(grad_gate_pre, gate_mat) + contract_last(grad_up_pre, up_mat)
    ).astype(jnp.bfloat16)
    return (hidden, expert_out, grad_gate_pre, grad_up_pre, pair_grad)


def local(tokens, expert_ids, gate_values, upstream, w_gate, w_up, w_down):
    local_tokens = tokens.shape[0]
    width = tokens.shape[1]
    top_count = expert_ids.shape[1]
    ff_width = w_gate.shape[2]
    outer_count = lax.axis_size("outer")
    inner_count = lax.axis_size("inner")
    expert_count = outer_count * inner_count
    capacity = min(local_tokens, 3 * local_tokens * top_count // (2 * expert_count))
    pair_count = local_tokens * top_count
    flat_ids = expert_ids.reshape(-1)
    flat_gates = gate_values.reshape(-1)
    onehot = (flat_ids[:, None] == jnp.arange(expert_count, dtype=jnp.int32)[None, :]).astype(
        jnp.int32
    )
    slot_rank = jnp.sum((jnp.cumsum(onehot, axis=0) - onehot) * onehot, axis=1)
    pair_slot = flat_ids * capacity + slot_rank
    slot_pair = (
        jnp.full((expert_count * capacity,), pair_count, jnp.int32)
        .at[pair_slot]
        .set(jnp.arange(pair_count, dtype=jnp.int32))
    )
    slot_token = jnp.where(slot_pair < pair_count, slot_pair // top_count, local_tokens)
    token_pad = jnp.concatenate([tokens, jnp.zeros((1, width), jnp.bfloat16)], axis=0)
    upstream_pad = jnp.concatenate([upstream, jnp.zeros((1, width), jnp.bfloat16)], axis=0)
    gate_pad = jnp.concatenate([flat_gates, jnp.zeros((1,), jnp.float32)], axis=0)
    fold = 1
    while (capacity * fold) % 16 or (width // fold) % 128 or width % fold:
        fold += 1
    if (width // fold) % 128 or width % fold:
        fold = 1
    narrow = width // fold
    flat_shape = (expert_count, capacity * fold, narrow)
    row_index = (slot_token[:, None] * fold + jnp.arange(fold, dtype=jnp.int32)[None, :]).reshape(-1)
    send_rows = token_pad.reshape(-1, narrow)[row_index]
    send_grads = (
        jnp.repeat(gate_pad[slot_pair], fold)[:, None]
        * upstream_pad.reshape(-1, narrow)[row_index].astype(jnp.float32)
    ).astype(jnp.bfloat16)
    got_rows, got_grads = (
        lax.all_to_all(
            send_rows.reshape(flat_shape),
            ("outer", "inner"),
            split_axis=0,
            concat_axis=0,
            tiled=True,
        ),
        lax.all_to_all(
            send_grads.reshape(flat_shape),
            ("outer", "inner"),
            split_axis=0,
            concat_axis=0,
            tiled=True,
        ),
    )
    rows_in = got_rows.reshape(-1, width)
    grads_in = got_grads.reshape(-1, width)
    dp_count = lax.axis_size("dp")
    piece = width // dp_count
    dp_index = lax.axis_index("dp")
    arrived = [lax.dynamic_slice_in_dim(rows_in, dp_index * piece, piece, axis=1)]
    for shift in range(1, dp_count):
        outgoing = lax.dynamic_slice_in_dim(rows_in, ((dp_index + shift) % dp_count) * piece, piece, axis=1)
        arrived.append(lax.ppermute(outgoing, "dp", [(j, (j + shift) % dp_count) for j in range(dp_count)]))
    rows_all = jnp.stack(arrived, axis=0)
    gate_mat, up_mat, down_mat = w_gate[0], w_up[0], w_down[0]
    gate_pre = jnp.dot(rows_in, gate_mat, preferred_element_type=jnp.float32)
    up_pre = jnp.dot(rows_in, up_mat, preferred_element_type=jnp.float32)
    sigma = jax.nn.sigmoid(gate_pre)
    silu_value = gate_pre * sigma
    hidden = (silu_value * up_pre).astype(jnp.bfloat16)
    expert_out = jnp.dot(hidden, down_mat, preferred_element_type=jnp.float32).astype(jnp.bfloat16)
    out_send = expert_out.reshape(flat_shape)
    grads_in, rows_all, out_send = lax.optimization_barrier((grads_in, rows_all, out_send))
    grad_hidden = contract_last(grads_in, down_mat)
    slope = sigma * (1.0 + gate_pre * (1.0 - sigma))
    grad_gate_pre = (grad_hidden * up_pre * slope).astype(jnp.bfloat16)
    grad_up_pre = (grad_hidden * silu_value).astype(jnp.bfloat16)
    pair_grad = (
        contract_last(grad_gate_pre, gate_mat) + contract_last(grad_up_pre, up_mat)
    ).astype(jnp.bfloat16)
    back_out, back_grad = (
        lax.all_to_all(
            out_send,
            ("outer", "inner"),
            split_axis=0,
            concat_axis=0,
            tiled=True,
        ),
        lax.all_to_all(
            pair_grad.reshape(flat_shape),
            ("outer", "inner"),
            split_axis=0,
            concat_axis=0,
            tiled=True,
        ),
    )
    joined_grads = jnp.concatenate([grad_gate_pre, grad_up_pre], axis=1)
    source_order = (dp_index - jnp.arange(dp_count)) % dp_count
    joined_all = jnp.take(lax.all_gather(joined_grads, "dp", axis=0, tiled=False), source_order, axis=0)
    grad_joined = lax.dot_general(
        rows_all, joined_all, (((0, 1), (0, 1)), ((), ())), preferred_element_type=jnp.float32
    )
    grads_arrived = [lax.dynamic_slice_in_dim(grads_in, dp_index * piece, piece, axis=1)]
    for shift in range(1, dp_count):
        outgoing = lax.dynamic_slice_in_dim(grads_in, ((dp_index + shift) % dp_count) * piece, piece, axis=1)
        grads_arrived.append(lax.ppermute(outgoing, "dp", [(j, (j + shift) % dp_count) for j in range(dp_count)]))
    grads_all = jnp.stack(grads_arrived, axis=0)
    hidden_all = jnp.take(lax.all_gather(hidden, "dp", axis=0, tiled=False), source_order, axis=0)
    grad_down = lax.dot_general(
        hidden_all, grads_all, (((0, 1), (0, 1)), ((), ())), preferred_element_type=jnp.float32
    )
    pair_index = (
        pair_slot.reshape(local_tokens, 1, top_count) * fold
        + jnp.arange(fold, dtype=jnp.int32)[None, :, None]
    ).reshape(local_tokens * fold, top_count)
    pair_out = back_out.reshape(-1, narrow)[pair_index].astype(jnp.float32)
    grad_w_gate = grad_joined[:, :ff_width].astype(jnp.bfloat16)[None]
    grad_w_up = grad_joined[:, ff_width:].astype(jnp.bfloat16)[None]
    grad_w_down = grad_down.astype(jnp.bfloat16)[None]
    grad_w_gate, grad_w_up, grad_w_down, back_grad = lax.optimization_barrier(
        (grad_w_gate, grad_w_up, grad_w_down, back_grad)
    )
    pair_back = back_grad.reshape(-1, narrow)[pair_index].astype(jnp.float32)
    gate_rows = jnp.repeat(gate_values, fold, axis=0)
    output = (
        jnp.sum(gate_rows[:, :, None] * pair_out, axis=1).reshape(local_tokens, width).astype(jnp.bfloat16)
    )
    grad_tokens = jnp.sum(pair_back, axis=1).reshape(local_tokens, width).astype(jnp.bfloat16)
    upstream_rows = upstream.reshape(local_tokens * fold, narrow).astype(jnp.float32)
    grad_gates = jnp.sum(
        jnp.sum(upstream_rows[:, None, :] * pair_out, axis=2).reshape(local_tokens, fold, top_count),
        axis=1,
    )
    return (output, grad_tokens, grad_gates, grad_w_gate, grad_w_up, grad_w_down)


def solution(mesh):
    placed = (
        P(("dp", "outer", "inner"), None),
        P(("dp", "outer", "inner"), None),
        P(("dp", "outer", "inner"), None),
        P(("dp", "outer", "inner"), None),
        P(("outer", "inner"), None, None),
        P(("outer", "inner"), None, None),
        P(("outer", "inner"), None, None),
    )
    return jax.shard_map(
        local,
        mesh=mesh,
        in_specs=placed,
        out_specs=(
            P(("dp", "outer", "inner"), None),
            P(("dp", "outer", "inner"), None),
            P(("dp", "outer", "inner"), None),
            P(("outer", "inner"), "dp", None),
            P(("outer", "inner"), "dp", None),
            P(("outer", "inner"), None, "dp"),
        ),
        check_vma=False,
    )
```

```python
import jax
import jax.numpy as jnp
from jax import lax
from jax.sharding import PartitionSpec as P


def contract_last(left, right):
    return lax.dot_general(
        left, right, (((1,), (1,)), ((), ())), preferred_element_type=jnp.float32
    )


def contract_first(left, right):
    return lax.dot_general(
        left, right, (((0,), (0,)), ((), ())), preferred_element_type=jnp.float32
    )


def expert_rows(rows_in, grads_in, gate_mat, up_mat, down_mat):
    gate_pre = jnp.dot(rows_in, gate_mat, preferred_element_type=jnp.float32)
    up_pre = jnp.dot(rows_in, up_mat, preferred_element_type=jnp.float32)
    sigma = jax.nn.sigmoid(gate_pre)
    silu_value = gate_pre * sigma
    hidden = (silu_value * up_pre).astype(jnp.bfloat16)
    expert_out = jnp.dot(hidden, down_mat, preferred_element_type=jnp.float32).astype(jnp.bfloat16)
    grad_hidden = contract_last(grads_in, down_mat)
    slope = sigma * (1.0 + gate_pre * (1.0 - sigma))
    grad_gate_pre = (grad_hidden * up_pre * slope).astype(jnp.bfloat16)
    grad_up_pre = (grad_hidden * silu_value).astype(jnp.bfloat16)
    pair_grad = (
        contract_last(grad_gate_pre, gate_mat) + contract_last(grad_up_pre, up_mat)
    ).astype(jnp.bfloat16)
    return (hidden, expert_out, grad_gate_pre, grad_up_pre, pair_grad)


def local(tokens, expert_ids, gate_values, upstream, w_gate, w_up, w_down):
    local_tokens = tokens.shape[0]
    width = tokens.shape[1]
    top_count = expert_ids.shape[1]
    ff_width = w_gate.shape[2]
    outer_count = lax.axis_size("outer")
    inner_count = lax.axis_size("inner")
    expert_count = outer_count * inner_count
    capacity = min(local_tokens, 3 * local_tokens * top_count // (2 * expert_count))
    pair_count = local_tokens * top_count
    flat_ids = expert_ids.reshape(-1)
    flat_gates = gate_values.reshape(-1)
    onehot = (flat_ids[:, None] == jnp.arange(expert_count, dtype=jnp.int32)[None, :]).astype(
        jnp.int32
    )
    slot_rank = jnp.sum((jnp.cumsum(onehot, axis=0) - onehot) * onehot, axis=1)
    pair_slot = flat_ids * capacity + slot_rank
    slot_pair = (
        jnp.full((expert_count * capacity,), pair_count, jnp.int32)
        .at[pair_slot]
        .set(jnp.arange(pair_count, dtype=jnp.int32))
    )
    slot_token = jnp.where(slot_pair < pair_count, slot_pair // top_count, local_tokens)
    token_pad = jnp.concatenate([tokens, jnp.zeros((1, width), jnp.bfloat16)], axis=0)
    upstream_pad = jnp.concatenate([upstream, jnp.zeros((1, width), jnp.bfloat16)], axis=0)
    gate_pad = jnp.concatenate([flat_gates, jnp.zeros((1,), jnp.float32)], axis=0)
    fold = 1
    while (capacity * fold) % 16 or (width // fold) % 128 or width % fold:
        fold += 1
    if (width // fold) % 128 or width % fold:
        fold = 1
    narrow = width // fold
    flat_shape = (expert_count, capacity * fold, narrow)
    row_index = (slot_token[:, None] * fold + jnp.arange(fold, dtype=jnp.int32)[None, :]).reshape(-1)
    send_rows = token_pad.reshape(-1, narrow)[row_index]
    send_grads = (
        jnp.repeat(gate_pad[slot_pair], fold)[:, None]
        * upstream_pad.reshape(-1, narrow)[row_index].astype(jnp.float32)
    ).astype(jnp.bfloat16)
    got_rows, got_grads = (
        lax.all_to_all(
            send_rows.reshape(flat_shape),
            ("outer", "inner"),
            split_axis=0,
            concat_axis=0,
            tiled=True,
        ),
        lax.all_to_all(
            send_grads.reshape(flat_shape),
            ("outer", "inner"),
            split_axis=0,
            concat_axis=0,
            tiled=True,
        ),
    )
    rows_in = got_rows.reshape(-1, width)
    grads_in = got_grads.reshape(-1, width)
    dp_count = lax.axis_size("dp")
    piece = width // dp_count
    dp_index = lax.axis_index("dp")
    arrived = [lax.dynamic_slice_in_dim(rows_in, dp_index * piece, piece, axis=1)]
    for shift in range(1, dp_count):
        outgoing = lax.dynamic_slice_in_dim(rows_in, ((dp_index + shift) % dp_count) * piece, piece, axis=1)
        arrived.append(lax.ppermute(outgoing, "dp", [(j, (j + shift) % dp_count) for j in range(dp_count)]))
    rows_all = jnp.stack(arrived, axis=0)
    gate_mat, up_mat, down_mat = w_gate[0], w_up[0], w_down[0]
    gate_pre = jnp.dot(rows_in, gate_mat, preferred_element_type=jnp.float32)
    up_pre = jnp.dot(rows_in, up_mat, preferred_element_type=jnp.float32)
    sigma = jax.nn.sigmoid(gate_pre)
    silu_value = gate_pre * sigma
    hidden = (silu_value * up_pre).astype(jnp.bfloat16)
    expert_out = jnp.dot(hidden, down_mat, preferred_element_type=jnp.float32).astype(jnp.bfloat16)
    out_send = expert_out.reshape(flat_shape)
    grads_in, rows_all, out_send = lax.optimization_barrier((grads_in, rows_all, out_send))
    grad_hidden = contract_last(grads_in, down_mat)
    slope = sigma * (1.0 + gate_pre * (1.0 - sigma))
    grad_gate_pre = (grad_hidden * up_pre * slope).astype(jnp.bfloat16)
    grad_up_pre = (grad_hidden * silu_value).astype(jnp.bfloat16)
    pair_grad = (
        contract_last(grad_gate_pre, gate_mat) + contract_last(grad_up_pre, up_mat)
    ).astype(jnp.bfloat16)
    back_out, back_grad = (
        lax.all_to_all(
            out_send,
            ("outer", "inner"),
            split_axis=0,
            concat_axis=0,
            tiled=True,
        ),
        lax.all_to_all(
            pair_grad.reshape(flat_shape),
            ("outer", "inner"),
            split_axis=0,
            concat_axis=0,
            tiled=True,
        ),
    )
    joined_grads = jnp.concatenate([grad_gate_pre, grad_up_pre], axis=1)
    source_order = (dp_index - jnp.arange(dp_count)) % dp_count
    joined_all = jnp.take(lax.all_gather(joined_grads, "dp", axis=0, tiled=False), source_order, axis=0)
    grad_joined = lax.dot_general(
        rows_all, joined_all, (((0, 1), (0, 1)), ((), ())), preferred_element_type=jnp.float32
    )
    grad_down = lax.psum_scatter(
        contract_first(hidden, grads_in).astype(jnp.bfloat16),
        "dp",
        scatter_dimension=1,
        tiled=True,
    ).astype(jnp.float32)
    pair_index = (
        pair_slot.reshape(local_tokens, 1, top_count) * fold
        + jnp.arange(fold, dtype=jnp.int32)[None, :, None]
    ).reshape(local_tokens * fold, top_count)
    pair_out = back_out.reshape(-1, narrow)[pair_index].astype(jnp.float32)
    grad_w_gate = grad_joined[:, :ff_width].astype(jnp.bfloat16)[None]
    grad_w_up = grad_joined[:, ff_width:].astype(jnp.bfloat16)[None]
    grad_w_gate, grad_w_up, back_grad = lax.optimization_barrier((grad_w_gate, grad_w_up, back_grad))
    pair_back = back_grad.reshape(-1, narrow)[pair_index].astype(jnp.float32)
    gate_rows = jnp.repeat(gate_values, fold, axis=0)
    output = (
        jnp.sum(gate_rows[:, :, None] * pair_out, axis=1).reshape(local_tokens, width).astype(jnp.bfloat16)
    )
    grad_tokens = jnp.sum(pair_back, axis=1).reshape(local_tokens, width).astype(jnp.bfloat16)
    upstream_rows = upstream.reshape(local_tokens * fold, narrow).astype(jnp.float32)
    grad_gates = jnp.sum(
        jnp.sum(upstream_rows[:, None, :] * pair_out, axis=2).reshape(local_tokens, fold, top_count),
        axis=1,
    )
    grad_w_down = grad_down.astype(jnp.bfloat16)[None]
    return (output, grad_tokens, grad_gates, grad_w_gate, grad_w_up, grad_w_down)


def solution(mesh):
    placed = (
        P(("dp", "outer", "inner"), None),
        P(("dp", "outer", "inner"), None),
        P(("dp", "outer", "inner"), None),
        P(("dp", "outer", "inner"), None),
        P(("outer", "inner"), None, None),
        P(("outer", "inner"), None, None),
        P(("outer", "inner"), None, None),
    )
    return jax.shard_map(
        local,
        mesh=mesh,
        in_specs=placed,
        out_specs=(
            P(("dp", "outer", "inner"), None),
            P(("dp", "outer", "inner"), None),
            P(("dp", "outer", "inner"), None),
            P(("outer", "inner"), "dp", None),
            P(("outer", "inner"), "dp", None),
            P(("outer", "inner"), None, "dp"),
        ),
        check_vma=False,
    )
```

```python
import jax
import jax.numpy as jnp
from jax import lax
from jax.sharding import PartitionSpec as P


def contract_last(left, right):
    return lax.dot_general(
        left, right, (((1,), (1,)), ((), ())), preferred_element_type=jnp.float32
    )


def contract_first(left, right):
    return lax.dot_general(
        left, right, (((0,), (0,)), ((), ())), preferred_element_type=jnp.float32
    )


def expert_rows(rows_in, grads_in, gate_mat, up_mat, down_mat):
    gate_pre = jnp.dot(rows_in, gate_mat, preferred_element_type=jnp.float32)
    up_pre = jnp.dot(rows_in, up_mat, preferred_element_type=jnp.float32)
    sigma = jax.nn.sigmoid(gate_pre)
    silu_value = gate_pre * sigma
    hidden = (silu_value * up_pre).astype(jnp.bfloat16)
    expert_out = jnp.dot(hidden, down_mat, preferred_element_type=jnp.float32).astype(jnp.bfloat16)
    grad_hidden = contract_last(grads_in, down_mat)
    slope = sigma * (1.0 + gate_pre * (1.0 - sigma))
    grad_gate_pre = (grad_hidden * up_pre * slope).astype(jnp.bfloat16)
    grad_up_pre = (grad_hidden * silu_value).astype(jnp.bfloat16)
    pair_grad = (
        contract_last(grad_gate_pre, gate_mat) + contract_last(grad_up_pre, up_mat)
    ).astype(jnp.bfloat16)
    return (hidden, expert_out, grad_gate_pre, grad_up_pre, pair_grad)


def local(tokens, expert_ids, gate_values, upstream, w_gate, w_up, w_down):
    local_tokens = tokens.shape[0]
    width = tokens.shape[1]
    top_count = expert_ids.shape[1]
    ff_width = w_gate.shape[2]
    outer_count = lax.axis_size("outer")
    inner_count = lax.axis_size("inner")
    expert_count = outer_count * inner_count
    capacity = min(local_tokens, 3 * local_tokens * top_count // (2 * expert_count))
    pair_count = local_tokens * top_count
    flat_ids = expert_ids.reshape(-1)
    flat_gates = gate_values.reshape(-1)
    onehot = (flat_ids[:, None] == jnp.arange(expert_count, dtype=jnp.int32)[None, :]).astype(
        jnp.int32
    )
    slot_rank = jnp.sum((jnp.cumsum(onehot, axis=0) - onehot) * onehot, axis=1)
    pair_slot = flat_ids * capacity + slot_rank
    slot_pair = (
        jnp.full((expert_count * capacity,), pair_count, jnp.int32)
        .at[pair_slot]
        .set(jnp.arange(pair_count, dtype=jnp.int32))
    )
    slot_token = jnp.where(slot_pair < pair_count, slot_pair // top_count, local_tokens)
    token_pad = jnp.concatenate([tokens, jnp.zeros((1, width), jnp.bfloat16)], axis=0)
    upstream_pad = jnp.concatenate([upstream, jnp.zeros((1, width), jnp.bfloat16)], axis=0)
    gate_pad = jnp.concatenate([flat_gates, jnp.zeros((1,), jnp.float32)], axis=0)
    fold = 1
    while (capacity * fold) % 16 or (width // fold) % 128 or width % fold:
        fold += 1
    if (width // fold) % 128 or width % fold:
        fold = 1
    narrow = width // fold
    flat_shape = (expert_count, capacity * fold, narrow)
    row_index = (slot_token[:, None] * fold + jnp.arange(fold, dtype=jnp.int32)[None, :]).reshape(-1)
    send_rows = token_pad.reshape(-1, narrow)[row_index]
    send_grads = (
        jnp.repeat(gate_pad[slot_pair], fold)[:, None]
        * upstream_pad.reshape(-1, narrow)[row_index].astype(jnp.float32)
    ).astype(jnp.bfloat16)
    got_rows, got_grads = (
        lax.all_to_all(
            send_rows.reshape(flat_shape),
            ("outer", "inner"),
            split_axis=0,
            concat_axis=0,
            tiled=True,
        ),
        lax.all_to_all(
            send_grads.reshape(flat_shape),
            ("outer", "inner"),
            split_axis=0,
            concat_axis=0,
            tiled=True,
        ),
    )
    rows_in = got_rows.reshape(-1, width)
    grads_in = got_grads.reshape(-1, width)
    dp_count = lax.axis_size("dp")
    piece = width // dp_count
    dp_index = lax.axis_index("dp")
    arrived = [lax.dynamic_slice_in_dim(rows_in, dp_index * piece, piece, axis=1)]
    for shift in range(1, dp_count):
        outgoing = lax.dynamic_slice_in_dim(rows_in, ((dp_index + shift) % dp_count) * piece, piece, axis=1)
        arrived.append(lax.ppermute(outgoing, "dp", [(j, (j + shift) % dp_count) for j in range(dp_count)]))
    gate_mat, up_mat, down_mat = w_gate[0], w_up[0], w_down[0]
    gate_pre = jnp.dot(rows_in, gate_mat, preferred_element_type=jnp.float32)
    up_pre = jnp.dot(rows_in, up_mat, preferred_element_type=jnp.float32)
    sigma = jax.nn.sigmoid(gate_pre)
    silu_value = gate_pre * sigma
    hidden = (silu_value * up_pre).astype(jnp.bfloat16)
    expert_out = jnp.dot(hidden, down_mat, preferred_element_type=jnp.float32).astype(jnp.bfloat16)
    out_send = expert_out.reshape(flat_shape)
    grads_in, arrived, out_send = lax.optimization_barrier((grads_in, arrived, out_send))
    rows_all = jnp.stack(arrived, axis=0)
    grad_hidden = contract_last(grads_in, down_mat)
    slope = sigma * (1.0 + gate_pre * (1.0 - sigma))
    grad_gate_pre = (grad_hidden * up_pre * slope).astype(jnp.bfloat16)
    grad_up_pre = (grad_hidden * silu_value).astype(jnp.bfloat16)
    pair_grad = (
        contract_last(grad_gate_pre, gate_mat) + contract_last(grad_up_pre, up_mat)
    ).astype(jnp.bfloat16)
    back_out, back_grad = (
        lax.all_to_all(
            out_send,
            ("outer", "inner"),
            split_axis=0,
            concat_axis=0,
            tiled=True,
        ),
        lax.all_to_all(
            pair_grad.reshape(flat_shape),
            ("outer", "inner"),
            split_axis=0,
            concat_axis=0,
            tiled=True,
        ),
    )
    joined_grads = jnp.concatenate([grad_gate_pre, grad_up_pre], axis=1)
    source_order = (dp_index - jnp.arange(dp_count)) % dp_count
    joined_all = jnp.take(lax.all_gather(joined_grads, "dp", axis=0, tiled=False), source_order, axis=0)
    grad_joined = lax.dot_general(
        rows_all, joined_all, (((0, 1), (0, 1)), ((), ())), preferred_element_type=jnp.float32
    )
    grad_down = lax.psum_scatter(
        contract_first(hidden, grads_in).astype(jnp.bfloat16),
        "dp",
        scatter_dimension=1,
        tiled=True,
    ).astype(jnp.float32)
    pair_index = (
        pair_slot.reshape(local_tokens, 1, top_count) * fold
        + jnp.arange(fold, dtype=jnp.int32)[None, :, None]
    ).reshape(local_tokens * fold, top_count)
    pair_out = back_out.reshape(-1, narrow)[pair_index].astype(jnp.float32)
    grad_w_gate = grad_joined[:, :ff_width].astype(jnp.bfloat16)[None]
    grad_w_up = grad_joined[:, ff_width:].astype(jnp.bfloat16)[None]
    grad_w_gate, grad_w_up, back_grad = lax.optimization_barrier((grad_w_gate, grad_w_up, back_grad))
    pair_back = back_grad.reshape(-1, narrow)[pair_index].astype(jnp.float32)
    gate_rows = jnp.repeat(gate_values, fold, axis=0)
    output = (
        jnp.sum(gate_rows[:, :, None] * pair_out, axis=1).reshape(local_tokens, width).astype(jnp.bfloat16)
    )
    grad_tokens = jnp.sum(pair_back, axis=1).reshape(local_tokens, width).astype(jnp.bfloat16)
    upstream_rows = upstream.reshape(local_tokens * fold, narrow).astype(jnp.float32)
    grad_gates = jnp.sum(
        jnp.sum(upstream_rows[:, None, :] * pair_out, axis=2).reshape(local_tokens, fold, top_count),
        axis=1,
    )
    grad_w_down = grad_down.astype(jnp.bfloat16)[None]
    return (output, grad_tokens, grad_gates, grad_w_gate, grad_w_up, grad_w_down)


def solution(mesh):
    placed = (
        P(("dp", "outer", "inner"), None),
        P(("dp", "outer", "inner"), None),
        P(("dp", "outer", "inner"), None),
        P(("dp", "outer", "inner"), None),
        P(("outer", "inner"), None, None),
        P(("outer", "inner"), None, None),
        P(("outer", "inner"), None, None),
    )
    return jax.shard_map(
        local,
        mesh=mesh,
        in_specs=placed,
        out_specs=(
            P(("dp", "outer", "inner"), None),
            P(("dp", "outer", "inner"), None),
            P(("dp", "outer", "inner"), None),
            P(("outer", "inner"), "dp", None),
            P(("outer", "inner"), "dp", None),
            P(("outer", "inner"), None, "dp"),
        ),
        check_vma=False,
    )
```

```python
import jax
import jax.numpy as jnp
from jax import lax
from jax.sharding import PartitionSpec as P


def contract_last(left, right):
    return lax.dot_general(
        left, right, (((1,), (1,)), ((), ())), preferred_element_type=jnp.float32
    )


def contract_first(left, right):
    return lax.dot_general(
        left, right, (((0,), (0,)), ((), ())), preferred_element_type=jnp.float32
    )


def expert_rows(rows_in, grads_in, gate_mat, up_mat, down_mat):
    gate_pre = jnp.dot(rows_in, gate_mat, preferred_element_type=jnp.float32)
    up_pre = jnp.dot(rows_in, up_mat, preferred_element_type=jnp.float32)
    sigma = jax.nn.sigmoid(gate_pre)
    silu_value = gate_pre * sigma
    hidden = (silu_value * up_pre).astype(jnp.bfloat16)
    expert_out = jnp.dot(hidden, down_mat, preferred_element_type=jnp.float32).astype(jnp.bfloat16)
    grad_hidden = contract_last(grads_in, down_mat)
    slope = sigma * (1.0 + gate_pre * (1.0 - sigma))
    grad_gate_pre = (grad_hidden * up_pre * slope).astype(jnp.bfloat16)
    grad_up_pre = (grad_hidden * silu_value).astype(jnp.bfloat16)
    pair_grad = (
        contract_last(grad_gate_pre, gate_mat) + contract_last(grad_up_pre, up_mat)
    ).astype(jnp.bfloat16)
    return (hidden, expert_out, grad_gate_pre, grad_up_pre, pair_grad)


def local(tokens, expert_ids, gate_values, upstream, w_gate, w_up, w_down):
    local_tokens = tokens.shape[0]
    width = tokens.shape[1]
    top_count = expert_ids.shape[1]
    ff_width = w_gate.shape[2]
    outer_count = lax.axis_size("outer")
    inner_count = lax.axis_size("inner")
    expert_count = outer_count * inner_count
    capacity = min(local_tokens, 3 * local_tokens * top_count // (2 * expert_count))
    pair_count = local_tokens * top_count
    flat_ids = expert_ids.reshape(-1)
    flat_gates = gate_values.reshape(-1)
    onehot = (flat_ids[:, None] == jnp.arange(expert_count, dtype=jnp.int32)[None, :]).astype(
        jnp.int32
    )
    slot_rank = jnp.sum((jnp.cumsum(onehot, axis=0) - onehot) * onehot, axis=1)
    pair_slot = flat_ids * capacity + slot_rank
    slot_pair = (
        jnp.full((expert_count * capacity,), pair_count, jnp.int32)
        .at[pair_slot]
        .set(jnp.arange(pair_count, dtype=jnp.int32))
    )
    slot_token = jnp.where(slot_pair < pair_count, slot_pair // top_count, local_tokens)
    token_pad = jnp.concatenate([tokens, jnp.zeros((1, width), jnp.bfloat16)], axis=0)
    upstream_pad = jnp.concatenate([upstream, jnp.zeros((1, width), jnp.bfloat16)], axis=0)
    gate_pad = jnp.concatenate([flat_gates, jnp.zeros((1,), jnp.float32)], axis=0)
    fold = 1
    while (capacity * fold) % 16 or (width // fold) % 128 or width % fold:
        fold += 1
    if (width // fold) % 128 or width % fold:
        fold = 1
    narrow = width // fold
    flat_shape = (expert_count, capacity * fold, narrow)
    row_index = (slot_token[:, None] * fold + jnp.arange(fold, dtype=jnp.int32)[None, :]).reshape(-1)
    token_view = token_pad.reshape(-1, narrow)
    picker = (row_index[:, None] == jnp.arange(token_view.shape[0], dtype=jnp.int32)[None, :]).astype(
        jnp.bfloat16
    )
    send_rows = jnp.dot(picker, token_view, preferred_element_type=jnp.float32).astype(jnp.bfloat16)
    send_grads = (
        jnp.repeat(gate_pad[slot_pair], fold)[:, None]
        * upstream_pad.reshape(-1, narrow)[row_index].astype(jnp.float32)
    ).astype(jnp.bfloat16)
    got_rows, got_grads = (
        lax.all_to_all(
            send_rows.reshape(flat_shape),
            ("outer", "inner"),
            split_axis=0,
            concat_axis=0,
            tiled=True,
        ),
        lax.all_to_all(
            send_grads.reshape(flat_shape),
            ("outer", "inner"),
            split_axis=0,
            concat_axis=0,
            tiled=True,
        ),
    )
    rows_in = got_rows.reshape(-1, width)
    grads_in = got_grads.reshape(-1, width)
    dp_count = lax.axis_size("dp")
    piece = width // dp_count
    dp_index = lax.axis_index("dp")
    arrived = [lax.dynamic_slice_in_dim(rows_in, dp_index * piece, piece, axis=1)]
    for shift in range(1, dp_count):
        outgoing = lax.dynamic_slice_in_dim(rows_in, ((dp_index + shift) % dp_count) * piece, piece, axis=1)
        arrived.append(lax.ppermute(outgoing, "dp", [(j, (j + shift) % dp_count) for j in range(dp_count)]))
    rows_all = jnp.stack(arrived, axis=0)
    gate_mat, up_mat, down_mat = w_gate[0], w_up[0], w_down[0]
    gate_pre = jnp.dot(rows_in, gate_mat, preferred_element_type=jnp.float32)
    up_pre = jnp.dot(rows_in, up_mat, preferred_element_type=jnp.float32)
    sigma = jax.nn.sigmoid(gate_pre)
    silu_value = gate_pre * sigma
    hidden = (silu_value * up_pre).astype(jnp.bfloat16)
    expert_out = jnp.dot(hidden, down_mat, preferred_element_type=jnp.float32).astype(jnp.bfloat16)
    out_send = expert_out.reshape(flat_shape)
    grads_in, rows_all, out_send = lax.optimization_barrier((grads_in, rows_all, out_send))
    grad_hidden = contract_last(grads_in, down_mat)
    slope = sigma * (1.0 + gate_pre * (1.0 - sigma))
    grad_gate_pre = (grad_hidden * up_pre * slope).astype(jnp.bfloat16)
    grad_up_pre = (grad_hidden * silu_value).astype(jnp.bfloat16)
    pair_grad = (
        contract_last(grad_gate_pre, gate_mat) + contract_last(grad_up_pre, up_mat)
    ).astype(jnp.bfloat16)
    back_out, back_grad = (
        lax.all_to_all(
            out_send,
            ("outer", "inner"),
            split_axis=0,
            concat_axis=0,
            tiled=True,
        ),
        lax.all_to_all(
            pair_grad.reshape(flat_shape),
            ("outer", "inner"),
            split_axis=0,
            concat_axis=0,
            tiled=True,
        ),
    )
    joined_grads = jnp.concatenate([grad_gate_pre, grad_up_pre], axis=1)
    source_order = (dp_index - jnp.arange(dp_count)) % dp_count
    joined_all = jnp.take(lax.all_gather(joined_grads, "dp", axis=0, tiled=False), source_order, axis=0)
    grad_joined = lax.dot_general(
        rows_all, joined_all, (((0, 1), (0, 1)), ((), ())), preferred_element_type=jnp.float32
    )
    grad_down = lax.psum_scatter(
        contract_first(hidden, grads_in).astype(jnp.bfloat16),
        "dp",
        scatter_dimension=1,
        tiled=True,
    ).astype(jnp.float32)
    pair_index = (
        pair_slot.reshape(local_tokens, 1, top_count) * fold
        + jnp.arange(fold, dtype=jnp.int32)[None, :, None]
    ).reshape(local_tokens * fold, top_count)
    pair_out = back_out.reshape(-1, narrow)[pair_index].astype(jnp.float32)
    grad_w_gate = grad_joined[:, :ff_width].astype(jnp.bfloat16)[None]
    grad_w_up = grad_joined[:, ff_width:].astype(jnp.bfloat16)[None]
    grad_w_gate, grad_w_up, back_grad = lax.optimization_barrier((grad_w_gate, grad_w_up, back_grad))
    pair_back = back_grad.reshape(-1, narrow)[pair_index].astype(jnp.float32)
    gate_rows = jnp.repeat(gate_values, fold, axis=0)
    output = (
        jnp.sum(gate_rows[:, :, None] * pair_out, axis=1).reshape(local_tokens, width).astype(jnp.bfloat16)
    )
    grad_tokens = jnp.sum(pair_back, axis=1).reshape(local_tokens, width).astype(jnp.bfloat16)
    upstream_rows = upstream.reshape(local_tokens * fold, narrow).astype(jnp.float32)
    grad_gates = jnp.sum(
        jnp.sum(upstream_rows[:, None, :] * pair_out, axis=2).reshape(local_tokens, fold, top_count),
        axis=1,
    )
    grad_w_down = grad_down.astype(jnp.bfloat16)[None]
    return (output, grad_tokens, grad_gates, grad_w_gate, grad_w_up, grad_w_down)


def solution(mesh):
    placed = (
        P(("dp", "outer", "inner"), None),
        P(("dp", "outer", "inner"), None),
        P(("dp", "outer", "inner"), None),
        P(("dp", "outer", "inner"), None),
        P(("outer", "inner"), None, None),
        P(("outer", "inner"), None, None),
        P(("outer", "inner"), None, None),
    )
    return jax.shard_map(
        local,
        mesh=mesh,
        in_specs=placed,
        out_specs=(
            P(("dp", "outer", "inner"), None),
            P(("dp", "outer", "inner"), None),
            P(("dp", "outer", "inner"), None),
            P(("outer", "inner"), "dp", None),
            P(("outer", "inner"), "dp", None),
            P(("outer", "inner"), None, "dp"),
        ),
        check_vma=False,
    )
```
